512 devices in a mesh: space: 32 (over x, y, z_hi), tm: 16 (over z_lo, core).
Axes of the slice: x: 4, y: 4, z: 16 (z_hi: 2, z_lo: 8; z = z_hi * 8 + z_lo), core: 2. Of those that a mesh axis runs over, the one named last changes fastest.
Arguments:
- lattice_field: float32 [64, 128, 2048], P('tm', 'space'), may hold values from -6 to 6
- parity: int32 [16, 32, 128], P('tm', 'space'), may hold values from 0 to 1
- block_list: int32 [16, 8], replicated, may hold values from 0 to 15, as said below
- w_embed: bfloat16 [256, 768], replicated, may hold values from -0.5 to 0.5
- b_embed: float32 [768], replicated, may hold values from -3 to 3
- gain_in: float32 [768], replicated, may hold values from 0.5 to 1.5
- w_qkv: bfloat16 [768, 2304], replicated, may hold values from -4 to 4
- gain_out: float32 [768], replicated, may hold values from 0.5 to 1.5
- w_head: bfloat16 [768, 512], replicated, may hold values from -0.21875 to 0.21875
- b_head: float32 [512], replicated, may hold values from -3 to 3
Outputs:
- new_field: float32 [64, 128, 2048], P('tm', 'space')
- action_density: float32 [64, 128, 2048], P('tm', 'space')
- time_link: float32 [64, 128, 2048], P('tm', 'space')
- slab_link: float32 [64, 128, 2048], P('tm', 'space')
- totals: float32 [2], replicated
The draws below stay inside these ranges and needn't reach their ends.
Inputs may be any that keep to these rules, and one draw needn't show every extreme that they name: `block_list`: row b lists 8 different block numbers, b among them.
All inputs are finite; a program needn't handle non-finite values.
Results may differ from the reference program's by a relative error of at most 0.006.
Values may be sent and summed in bfloat16 or wider, within the bound.
No kernel may reach another device: no remote copies, remote signals or barrier semaphores. Data moves between devices by JAX's collectives and lax.ppermute only.
A program may use at most 64 MiB of HBM per device.

```python
import math
import jax
import jax.numpy as jnp
from jax import lax

P_SIZE = 4
D = 768
HEADS = 12
HS = 64
LY = 32
LZ = 64
BLK = 128
KSEL = 8
PATCH = 256
TOKD = 128
LT = 64
LX = 128
NB = 16
SITES = 16777216


def draw_lattice_field(key, part):
    second_key = jax.random.fold_in(key, 1)
    along_x = 0.6 + 1.2 * jnp.arange(LX, dtype=jnp.float32) / LX
    values = jax.random.normal(second_key, (LT, LX, LY * LZ), jnp.float32) * along_x[None, :, None]
    return jnp.clip(values, -6.0, 6.0)


def draw_block_list(key, part):
    rows_idx = jnp.arange(NB, dtype=jnp.int32)[:, None]
    cols_idx = jnp.arange(NB, dtype=jnp.int32)[None, :]
    blocks_dev = TOKD // BLK
    distance = (cols_idx - rows_idx) % NB
    near = (distance == 1) | (distance == NB - 1) | (distance == NB // 2)
    priority = jnp.where(distance == 0, 3, jnp.where(near, 2, jnp.where(cols_idx % blocks_dev == rows_idx % blocks_dev, 1, 0)))
    order_keys = jax.random.split(key, NB)
    ordering = jax.vmap(lambda row_key: jax.random.permutation(row_key, NB))(order_keys).astype(jnp.int32)
    ranking = priority.astype(jnp.int32) * NB + ordering
    _, chosen = lax.top_k(ranking, KSEL)
    return chosen.astype(jnp.int32)


def draw_w_qkv(key, part):
    first_key = jax.random.fold_in(key, 0)
    values = jax.random.normal(first_key, (D, 3 * D), jnp.float32) / D ** 0.5
    limit = min(6.0 / D ** 0.5, 4.0)
    values = jnp.clip(values, -limit, limit)
    return jnp.concatenate([values[:, :2 * D], 4.0 * values[:, 2 * D:]], axis=1).astype(jnp.bfloat16)


def plant(entries, rng, smallest, high):
    extent = entries.shape
    index_at = [jax.random.randint(jax.random.fold_in(rng, axis), (), 0, extent[axis]) for axis in range(len(extent))]
    entries = entries.at[tuple(index_at)].set(smallest)
    longest = extent.index(max(extent))
    index_at[longest] = (index_at[longest] + 1) % extent[longest]
    return entries.at[tuple(index_at)].set(high)


def noise(key, extent, scale, most, kind=jnp.bfloat16):
    return jnp.clip(scale * jax.random.normal(key, extent, jnp.float32), -most, most).astype(kind)


def setup_inputs(seed: int = 0) -> dict:
    streams_of = jax.random.split(jax.random.key(seed), 11)
    return {
        "lattice_field": draw_lattice_field(jax.random.fold_in(streams_of[10], 71), 0),
        "parity": plant(jax.random.randint(streams_of[1], (LT // P_SIZE, LX // P_SIZE, TOKD), 0, 2), jax.random.fold_in(streams_of[1], 1), 0, 1).astype(jnp.int32),
        "block_list": draw_block_list(jax.random.fold_in(streams_of[10], 71), 0),
        "w_embed": noise(streams_of[3], (PATCH, D), (PATCH // 2) ** -0.5, 0.5),
        "b_embed": noise(streams_of[4], (D,), 0.5, 3.0, jnp.float32),
        "gain_in": jnp.clip(jax.random.uniform(streams_of[5], (D,), jnp.float32, 0.5, 1.5), 0.5, 1.5),
        "w_qkv": draw_w_qkv(jax.random.fold_in(streams_of[10], 71), 0),
        "gain_out": jnp.clip(jax.random.uniform(streams_of[7], (D,), jnp.float32, 0.5, 1.5), 0.5, 1.5),
        "w_head": noise(streams_of[8], (D, 2 * PATCH), D ** -0.5, 0.21875),
        "b_head": noise(streams_of[9], (2 * PATCH,), 0.5, 3.0, jnp.float32),
    }


hopping = 0.2
quartic = 0.5
epsilon = 1e-05
log_two_pi = math.log(2.0 * math.pi)

def layer_norm(values, gain_vec):
    centre = values - lax.optimization_barrier(jnp.mean(values, axis=-1, keepdims=True))
    spread = lax.optimization_barrier(jnp.mean(centre * centre, axis=-1, keepdims=True))
    return centre * lax.rsqrt(spread + epsilon) * gain_vec

def site_parity():
    positions = jnp.arange(PATCH, dtype=jnp.int32)
    return (positions // P_SIZE ** 3 + positions // P_SIZE ** 2 % P_SIZE + positions // P_SIZE % P_SIZE + positions % P_SIZE) % 2

def reference(lattice_field, parity, block_list, w_embed, b_embed, gain_in, w_qkv, gain_out, w_head, b_head):
    lattice_grid = lattice_field.reshape(LT // P_SIZE, P_SIZE, LX // P_SIZE, P_SIZE, LY // P_SIZE, P_SIZE, LZ // P_SIZE, P_SIZE)
    slab_rows = lattice_grid.transpose(2, 0, 4, 6, 1, 3, 5, 7).reshape(LX // P_SIZE, LT // P_SIZE * TOKD, PATCH)
    slab_bits = parity.transpose(1, 0, 2).reshape(LX // P_SIZE, LT // P_SIZE * TOKD)
    pattern = site_parity()
    scale_factor = HS ** (-0.5)

    def one_slab(item_pair):
        site_rows, bits = item_pair
        frozen = pattern[None, :] == bits[:, None]
        frozen_in = jnp.where(frozen, site_rows, 0.0).astype(jnp.bfloat16)
        embedded = jnp.dot(frozen_in, w_embed, preferred_element_type=jnp.float32) + b_embed
        normed = layer_norm(embedded, gain_in).astype(jnp.bfloat16)
        qkv_rows = jnp.dot(normed, w_qkv, preferred_element_type=jnp.float32).astype(jnp.bfloat16)
        queries = qkv_rows[:, :D].reshape(NB, BLK, HEADS, HS)
        key_all = qkv_rows[:, D:2 * D].reshape(NB, BLK, HEADS, HS)
        value_all = qkv_rows[:, 2 * D:].reshape(NB, BLK, HEADS, HS)
        key_sel = key_all[block_list].reshape(NB, KSEL * BLK, HEADS, HS)
        value_sel = value_all[block_list].reshape(NB, KSEL * BLK, HEADS, HS)
        scores = jnp.einsum('bqhd,bkhd->bhqk', queries.astype(jnp.float32), key_sel.astype(jnp.float32)) * scale_factor
        row_top = lax.optimization_barrier(jnp.max(scores, axis=-1, keepdims=True))
        exp_scores = jnp.exp(scores - row_top)
        row_total = lax.optimization_barrier(jnp.sum(exp_scores, axis=-1))
        weights = exp_scores.astype(jnp.bfloat16)
        mixed = jnp.einsum('bhqk,bkhd->bqhd', weights.astype(jnp.float32), value_sel.astype(jnp.float32))
        mixed = mixed / row_total.transpose(0, 2, 1)[..., None]
        hidden = embedded + mixed.reshape(NB * BLK, D)
        normed_out = layer_norm(hidden, gain_out).astype(jnp.bfloat16)
        affine = jnp.dot(normed_out, w_head, preferred_element_type=jnp.float32) + b_head
        scale_log = jnp.tanh(affine[:, :PATCH])
        shift_val = affine[:, PATCH:]
        moved = jnp.where(frozen, site_rows, site_rows * jnp.exp(scale_log) + shift_val)
        log_det = jnp.sum(jnp.where(frozen, 0.0, scale_log))
        return (moved, log_det)
    moved_all, log_dets = lax.map(one_slab, (slab_rows, slab_bits))
    moved_grid = moved_all.reshape(LX // P_SIZE, LT // P_SIZE, LY // P_SIZE, LZ // P_SIZE, P_SIZE, P_SIZE, P_SIZE, P_SIZE)
    new_field = moved_grid.transpose(1, 4, 0, 5, 2, 6, 3, 7).reshape(LT, LX, LY * LZ)
    cube = new_field.reshape(LT, LX, LY, LZ)
    ahead_t = jnp.roll(cube, -1, 0)
    ahead_x = jnp.roll(cube, -1, 1)
    neighbours = ahead_t + ahead_x
    neighbours = neighbours + jnp.roll(cube, -1, 2)
    neighbours = neighbours + jnp.roll(cube, -1, 3)
    squared = cube * cube
    density = -2.0 * hopping * cube * neighbours + squared + quartic * (squared - 1.0) * (squared - 1.0)
    action_density = density.reshape(LT, LX, LY * LZ)
    time_link = (cube * ahead_t).reshape(LT, LX, LY * LZ)
    slab_link = (cube * ahead_x).reshape(LT, LX, LY * LZ)
    sum_log = -0.5 * jnp.sum(lattice_field * lattice_field) - jnp.sum(log_dets)
    sum_act = jnp.sum(action_density)
    totals = jnp.stack([sum_log / SITES - 0.5 * log_two_pi, sum_act / SITES]).astype(jnp.float32)
    return (new_field, action_density, time_link, slab_link, totals)
```

```python
import math

import numpy as np
import jax
import jax.numpy as jnp
from jax import lax
from jax.sharding import PartitionSpec as P

P_SIZE = 4
D = 768
HEADS = 12
HS = 64
LY = 32
LZ = 64
BLK = 128


hopping = 0.2
quartic = 0.5
epsilon = 1e-05
log_two_pi = math.log(2.0 * math.pi)


def shifted(x, axis, by):
    length = lax.axis_size(axis)
    return lax.ppermute(x, axis, [(i, (i + by) % length) for i in range(length)])


def layer_norm(values, gain_vec):
    centre = values - jnp.mean(values, axis=-1, keepdims=True)
    spread = jnp.mean(centre * centre, axis=-1, keepdims=True)
    return centre * lax.rsqrt(spread + epsilon) * gain_vec


def site_parity(patch_side):
    positions = np.arange(patch_side**4, dtype=np.int32)
    return (
        positions // patch_side**3
        + positions // patch_side**2 % patch_side
        + positions // patch_side % patch_side
        + positions % patch_side
    ) % 2


def packed_rows(p_bit):
    th, x4, y4, z4 = np.meshgrid(np.arange(2), np.arange(4), np.arange(4), np.arange(4), indexing="ij")
    t4 = 2 * th + (p_bit + x4 + y4 + z4) % 2
    return (((t4 * 4 + x4) * 4 + y4) * 4 + z4).reshape(-1)


def embed_packed(tokens, bits, w_pair, b_embed):
    both = jnp.dot(tokens, w_pair, preferred_element_type=jnp.float32)
    half = both.shape[-1] // 2
    return jnp.where(bits[..., None] > 0.5, both[..., half:], both[..., :half]) + b_embed


def shards(
    lattice_field, parity, block_list, w_embed, b_embed, gain_in, w_qkv, gain_out, w_head, b_head
):
    n_y = LY // P_SIZE
    n_z = LZ // P_SIZE
    tokens_dev = n_y * n_z
    patch_len = P_SIZE**4
    u = lattice_field
    bits = parity.reshape(n_y, n_z)

    lane = lax.broadcasted_iota(jnp.int32, u.shape, 2)
    t_pos = lax.broadcasted_iota(jnp.int32, u.shape, 0)
    x_pos = lax.broadcasted_iota(jnp.int32, u.shape, 1)
    site_bit = (t_pos + x_pos + lane // LZ + lane % LZ) % 2
    bits_lat = jnp.repeat(jnp.repeat(bits, P_SIZE, axis=0), P_SIZE, axis=1).reshape(LY * LZ)
    frozen = site_bit == bits_lat[None, None, :]
    frozen_in = jnp.where(frozen, u, 0.0).astype(jnp.bfloat16)

    packed = frozen_in[0::2] + frozen_in[1::2]
    tokens = (
        packed.reshape(2, P_SIZE, n_y, P_SIZE, n_z, P_SIZE)
        .transpose(2, 4, 0, 1, 3, 5)
        .reshape(tokens_dev, patch_len // 2)
    )
    bits_f = bits.reshape(1, tokens_dev).astype(jnp.bfloat16)
    send = jnp.concatenate([tokens, bits_f], axis=0)
    gathered = lax.all_gather(send, "tm", axis=0, tiled=True).reshape(-1, tokens_dev + 1, patch_len // 2)

    w_pair = jnp.concatenate(
        [w_embed[packed_rows(0)], w_embed[packed_rows(1)]], axis=1
    )
    bits_own = bits.reshape(tokens_dev).astype(jnp.float32)
    embedded = embed_packed(tokens, bits_own, w_pair, b_embed)
    normed = layer_norm(embedded, gain_in).astype(jnp.bfloat16)
    queries = jnp.dot(normed, w_qkv[:, :D], preferred_element_type=jnp.float32).astype(
        jnp.bfloat16
    )

    block_rows = lax.dynamic_index_in_dim(block_list, lax.axis_index("tm"), 0, keepdims=False)
    chosen = jnp.take(gathered, block_rows, axis=0)
    n_sel = chosen.shape[0]
    sel_tokens = chosen[:, :tokens_dev, :].reshape(n_sel * tokens_dev, patch_len // 2)
    sel_bits = chosen[:, tokens_dev, :].reshape(n_sel * tokens_dev).astype(jnp.float32)
    sel_embedded = embed_packed(sel_tokens, sel_bits, w_pair, b_embed)
    sel_normed = layer_norm(sel_embedded, gain_in).astype(jnp.bfloat16)
    kv = jnp.dot(sel_normed, w_qkv[:, D:], preferred_element_type=jnp.float32).astype(
        jnp.bfloat16
    )
    keys = kv[:, :D].reshape(n_sel * tokens_dev, HEADS, HS)
    values = kv[:, D:].reshape(n_sel * tokens_dev, HEADS, HS)

    scores = jnp.einsum(
        "qhd,khd->hqk",
        queries.reshape(tokens_dev, HEADS, HS),
        keys,
        preferred_element_type=jnp.float32,
    ) * HS ** (-0.5)
    row_top = jnp.max(scores, axis=-1, keepdims=True)
    exp_scores = jnp.exp(scores - row_top)
    row_total = jnp.sum(exp_scores, axis=-1)
    product = jnp.einsum(
        "hqk,khd->qhd",
        exp_scores.astype(jnp.bfloat16),
        values,
        preferred_element_type=jnp.float32,
    )
    mixed = (product / row_total.T[:, :, None]).reshape(tokens_dev, D)
    hidden = embedded + mixed
    normed_out = layer_norm(hidden, gain_out).astype(jnp.bfloat16)
    affine = jnp.dot(normed_out, w_head, preferred_element_type=jnp.float32) + b_head
    scale_log = jnp.tanh(affine[:, :patch_len])
    frozen_tok = jnp.asarray(site_parity(P_SIZE))[None, :] == bits.reshape(tokens_dev)[:, None]
    log_det = jnp.sum(jnp.where(frozen_tok, 0.0, scale_log))

    coupling = jnp.concatenate([scale_log, affine[:, patch_len:]], axis=1)
    coupling_lat = (
        coupling.reshape(n_y, n_z, 2, P_SIZE, P_SIZE, P_SIZE, P_SIZE)
        .transpose(2, 3, 4, 0, 5, 1, 6)
        .reshape(2, P_SIZE, P_SIZE, LY * LZ)
    )
    scale_lat = coupling_lat[0]
    shift_lat = coupling_lat[1]
    new_field = jnp.where(frozen, u, u * jnp.exp(scale_lat) + shift_lat)

    ahead_time = shifted(new_field[0:1].astype(jnp.bfloat16), "tm", -1).astype(jnp.float32)
    ahead_slab = shifted(new_field[:, 0:1].astype(jnp.bfloat16), "space", -1).astype(jnp.float32)
    next_time_field = jnp.concatenate([new_field[1:], ahead_time], axis=0)
    next_slab_field = jnp.concatenate([new_field[:, 1:], ahead_slab], axis=1)
    next_y_field = jnp.roll(new_field, -LZ, axis=2)
    next_z_field = jnp.where(
        lane % LZ == LZ - 1, jnp.roll(new_field, LZ - 1, axis=2), jnp.roll(new_field, -1, axis=2)
    )
    neighbours = next_time_field + next_slab_field
    neighbours = neighbours + next_y_field
    neighbours = neighbours + next_z_field
    squared = new_field * new_field
    density = (
        -2.0 * hopping * new_field * neighbours
        + squared
        + quartic * (squared - 1.0) * (squared - 1.0)
    )
    time_link = new_field * next_time_field
    slab_link = new_field * next_slab_field
    local_log = -0.5 * jnp.sum(u * u) - log_det
    local_act = jnp.sum(density)
    sum_log, sum_act = lax.psum(lax.psum((local_log, local_act), "tm"), "space")
    site_count = u.size * lax.axis_size("space") * lax.axis_size("tm")
    totals = jnp.stack([sum_log / site_count - 0.5 * log_two_pi, sum_act / site_count]).astype(
        jnp.float32
    )
    return (new_field, density, time_link, slab_link, totals)


def solution(mesh):
    in_specs = (
        P("tm", "space", None),
        P("tm", "space", None),
        P(),
        P(),
        P(),
        P(),
        P(),
        P(),
        P(),
        P(),
    )
    out_specs = (
        P("tm", "space", None),
        P("tm", "space", None),
        P("tm", "space", None),
        P("tm", "space", None),
        P(),
    )
    return jax.shard_map(shards, mesh=mesh, in_specs=in_specs, out_specs=out_specs, check_vma=False)
```

```python
import math

import numpy as np
import jax
import jax.numpy as jnp
from jax import lax
from jax.sharding import PartitionSpec as P

P_SIZE = 4
D = 768
HEADS = 12
HS = 64
LY = 32
LZ = 64
BLK = 128


hopping = 0.2
quartic = 0.5
epsilon = 1e-05
log_two_pi = math.log(2.0 * math.pi)


def exchange(x, axis, bit):
    length = lax.axis_size(axis)
    return lax.ppermute(x, axis, [(i, i ^ bit) for i in range(length)])


def doubling_sum(x, axis):
    bit = 1
    while bit < lax.axis_size(axis):
        x = x + exchange(x, axis, bit)
        bit *= 2
    return x


def doubling_gather(x, axis):
    bits = []
    bit = 1
    while bit < lax.axis_size(axis):
        bits.append(bit)
        bit *= 2
    offsets = [0]
    for bit in reversed(bits):
        x = jnp.concatenate([x, exchange(x, axis, bit)], axis=0)
        offsets = offsets + [o ^ bit for o in offsets]
    return x, offsets


def shifted(x, axis, by):
    length = lax.axis_size(axis)
    return lax.ppermute(x, axis, [(i, (i + by) % length) for i in range(length)])


def layer_norm(values, gain_vec):
    centre = values - jnp.mean(values, axis=-1, keepdims=True)
    spread = jnp.mean(centre * centre, axis=-1, keepdims=True)
    return centre * lax.rsqrt(spread + epsilon) * gain_vec


def site_parity(patch_side):
    positions = np.arange(patch_side**4, dtype=np.int32)
    return (
        positions // patch_side**3
        + positions // patch_side**2 % patch_side
        + positions // patch_side % patch_side
        + positions % patch_side
    ) % 2


def packed_rows(p_bit):
    th, x4, y4, z4 = np.meshgrid(np.arange(2), np.arange(4), np.arange(4), np.arange(4), indexing="ij")
    t4 = 2 * th + (p_bit + x4 + y4 + z4) % 2
    return (((t4 * 4 + x4) * 4 + y4) * 4 + z4).reshape(-1)


def embed_packed(tokens, bits, w_pair, b_embed):
    both = jnp.dot(tokens, w_pair, preferred_element_type=jnp.float32)
    half = both.shape[-1] // 2
    return jnp.where(bits[..., None] > 0.5, both[..., half:], both[..., :half]) + b_embed


def shards(
    lattice_field, parity, block_list, w_embed, b_embed, gain_in, w_qkv, gain_out, w_head, b_head
):
    n_y = LY // P_SIZE
    n_z = LZ // P_SIZE
    tokens_dev = n_y * n_z
    patch_len = P_SIZE**4
    u = lattice_field
    bits = parity.reshape(n_y, n_z)

    lane = lax.broadcasted_iota(jnp.int32, u.shape, 2)
    t_pos = lax.broadcasted_iota(jnp.int32, u.shape, 0)
    x_pos = lax.broadcasted_iota(jnp.int32, u.shape, 1)
    site_bit = (t_pos + x_pos + lane // LZ + lane % LZ) % 2
    bits_lat = jnp.repeat(jnp.repeat(bits, P_SIZE, axis=0), P_SIZE, axis=1).reshape(LY * LZ)
    frozen = site_bit == bits_lat[None, None, :]
    frozen_in = jnp.where(frozen, u, 0.0).astype(jnp.bfloat16)

    packed = frozen_in[0::2] + frozen_in[1::2]
    tokens = (
        packed.reshape(2, P_SIZE, n_y, P_SIZE, n_z, P_SIZE)
        .transpose(2, 4, 0, 1, 3, 5)
        .reshape(tokens_dev, patch_len // 2)
    )
    bits_f = bits.reshape(1, tokens_dev).astype(jnp.bfloat16)
    send = jnp.concatenate([tokens, bits_f], axis=0)
    gathered, offsets = doubling_gather(send[None], "tm")
    slot_of = np.argsort(np.asarray(offsets)).astype(np.int32)

    w_pair = jnp.concatenate(
        [w_embed[packed_rows(0)], w_embed[packed_rows(1)]], axis=1
    )
    bits_own = bits.reshape(tokens_dev).astype(jnp.float32)
    embedded = embed_packed(tokens, bits_own, w_pair, b_embed)
    normed = layer_norm(embedded, gain_in).astype(jnp.bfloat16)
    queries = jnp.dot(normed, w_qkv[:, :D], preferred_element_type=jnp.float32).astype(
        jnp.bfloat16
    )

    block_rows = lax.dynamic_index_in_dim(block_list, lax.axis_index("tm"), 0, keepdims=False)
    own = lax.axis_index("tm")
    chosen = jnp.take(gathered, jnp.asarray(slot_of)[block_rows ^ own], axis=0)
    n_sel = chosen.shape[0]
    sel_tokens = chosen[:, :tokens_dev, :].reshape(n_sel * tokens_dev, patch_len // 2)
    sel_bits = chosen[:, tokens_dev, :].reshape(n_sel * tokens_dev).astype(jnp.float32)
    sel_embedded = embed_packed(sel_tokens, sel_bits, w_pair, b_embed)
    sel_normed = layer_norm(sel_embedded, gain_in).astype(jnp.bfloat16)
    kv = jnp.dot(sel_normed, w_qkv[:, D:], preferred_element_type=jnp.float32).astype(
        jnp.bfloat16
    )
    keys = kv[:, :D].reshape(n_sel * tokens_dev, HEADS, HS)
    values = kv[:, D:].reshape(n_sel * tokens_dev, HEADS, HS)

    scores = jnp.einsum(
        "qhd,khd->hqk",
        queries.reshape(tokens_dev, HEADS, HS),
        keys,
        preferred_element_type=jnp.float32,
    ) * HS ** (-0.5)
    row_top = jnp.max(scores, axis=-1, keepdims=True)
    exp_scores = jnp.exp(scores - row_top)
    row_total = jnp.sum(exp_scores, axis=-1)
    product = jnp.einsum(
        "hqk,khd->qhd",
        exp_scores.astype(jnp.bfloat16),
        values,
        preferred_element_type=jnp.float32,
    )
    mixed = (product / row_total.T[:, :, None]).reshape(tokens_dev, D)
    hidden = embedded + mixed
    normed_out = layer_norm(hidden, gain_out).astype(jnp.bfloat16)
    affine = jnp.dot(normed_out, w_head, preferred_element_type=jnp.float32) + b_head
    scale_log = jnp.tanh(affine[:, :patch_len])
    frozen_tok = jnp.asarray(site_parity(P_SIZE))[None, :] == bits.reshape(tokens_dev)[:, None]
    log_det = jnp.sum(jnp.where(frozen_tok, 0.0, scale_log))

    coupling = jnp.concatenate([scale_log, affine[:, patch_len:]], axis=1)
    coupling_lat = (
        coupling.reshape(n_y, n_z, 2, P_SIZE, P_SIZE, P_SIZE, P_SIZE)
        .transpose(2, 3, 4, 0, 5, 1, 6)
        .reshape(2, P_SIZE, P_SIZE, LY * LZ)
    )
    scale_lat = coupling_lat[0]
    shift_lat = coupling_lat[1]
    new_field = jnp.where(frozen, u, u * jnp.exp(scale_lat) + shift_lat)

    ahead_time = shifted(new_field[0:1].astype(jnp.bfloat16), "tm", -1).astype(jnp.float32)
    ahead_slab = shifted(new_field[:, 0:1].astype(jnp.bfloat16), "space", -1).astype(jnp.float32)
    next_time_field = jnp.concatenate([new_field[1:], ahead_time], axis=0)
    next_slab_field = jnp.concatenate([new_field[:, 1:], ahead_slab], axis=1)
    next_y_field = jnp.roll(new_field, -LZ, axis=2)
    next_z_field = jnp.where(
        lane % LZ == LZ - 1, jnp.roll(new_field, LZ - 1, axis=2), jnp.roll(new_field, -1, axis=2)
    )
    neighbours = next_time_field + next_slab_field
    neighbours = neighbours + next_y_field
    neighbours = neighbours + next_z_field
    squared = new_field * new_field
    density = (
        -2.0 * hopping * new_field * neighbours
        + squared
        + quartic * (squared - 1.0) * (squared - 1.0)
    )
    time_link = new_field * next_time_field
    slab_link = new_field * next_slab_field
    local_log = -0.5 * jnp.sum(u * u) - log_det
    local_act = jnp.sum(density)
    sums = doubling_sum(doubling_sum(jnp.stack([local_log, local_act]), "tm"), "space")
    sum_log, sum_act = sums[0], sums[1]
    site_count = u.size * lax.axis_size("space") * lax.axis_size("tm")
    totals = jnp.stack([sum_log / site_count - 0.5 * log_two_pi, sum_act / site_count]).astype(
        jnp.float32
    )
    return (new_field, density, time_link, slab_link, totals)


def solution(mesh):
    in_specs = (
        P("tm", "space", None),
        P("tm", "space", None),
        P(),
        P(),
        P(),
        P(),
        P(),
        P(),
        P(),
        P(),
    )
    out_specs = (
        P("tm", "space", None),
        P("tm", "space", None),
        P("tm", "space", None),
        P("tm", "space", None),
        P(),
    )
    return jax.shard_map(shards, mesh=mesh, in_specs=in_specs, out_specs=out_specs, check_vma=False)
```

```python
import math

import numpy as np
import jax
import jax.numpy as jnp
from jax import lax
from jax.sharding import PartitionSpec as P

P_SIZE = 4
D = 768
HEADS = 12
HS = 64
LY = 32
LZ = 64
BLK = 128


hopping = 0.2
quartic = 0.5
epsilon = 1e-05
log_two_pi = math.log(2.0 * math.pi)


def exchange(x, axis, bit):
    length = lax.axis_size(axis)
    return lax.ppermute(x, axis, [(i, i ^ bit) for i in range(length)])


def doubling_sum(x, axis):
    bit = 1
    while bit < lax.axis_size(axis):
        x = x + exchange(x, axis, bit)
        bit *= 2
    return x


def doubling_gather(x, axis):
    bits = []
    bit = 1
    while bit < lax.axis_size(axis):
        bits.append(bit)
        bit *= 2
    offsets = [0]
    for bit in reversed(bits):
        x = jnp.concatenate([x, exchange(x, axis, bit)], axis=0)
        offsets = offsets + [o ^ bit for o in offsets]
    return x, offsets


def shifted(x, axis, by):
    length = lax.axis_size(axis)
    return lax.ppermute(x, axis, [(i, (i + by) % length) for i in range(length)])


def layer_norm(values, gain_vec):
    centre = values - jnp.mean(values, axis=-1, keepdims=True)
    spread = jnp.mean(centre * centre, axis=-1, keepdims=True)
    return centre * lax.rsqrt(spread + epsilon) * gain_vec


def site_parity(patch_side):
    positions = np.arange(patch_side**4, dtype=np.int32)
    return (
        positions // patch_side**3
        + positions // patch_side**2 % patch_side
        + positions // patch_side % patch_side
        + positions % patch_side
    ) % 2


def packed_rows(p_bit):
    th, x4, y4, z4 = np.meshgrid(np.arange(2), np.arange(4), np.arange(4), np.arange(4), indexing="ij")
    t4 = 2 * th + (p_bit + x4 + y4 + z4) % 2
    return (((t4 * 4 + x4) * 4 + y4) * 4 + z4).reshape(-1)


def embed_packed(tokens, bits, w_pair, b_embed):
    both = jnp.dot(tokens, w_pair, preferred_element_type=jnp.float32)
    half = both.shape[-1] // 2
    return jnp.where(bits[..., None] > 0.5, both[..., half:], both[..., :half]) + b_embed


def shards(
    lattice_field, parity, block_list, w_embed, b_embed, gain_in, w_qkv, gain_out, w_head, b_head
):
    n_y = LY // P_SIZE
    n_z = LZ // P_SIZE
    tokens_dev = n_y * n_z
    patch_len = P_SIZE**4
    u = lattice_field
    bits = parity.reshape(n_y, n_z)

    lane = lax.broadcasted_iota(jnp.int32, u.shape, 2)
    t_pos = lax.broadcasted_iota(jnp.int32, u.shape, 0)
    x_pos = lax.broadcasted_iota(jnp.int32, u.shape, 1)
    site_bit = (t_pos + x_pos + lane // LZ + lane % LZ) % 2
    bits_lat = jnp.repeat(jnp.repeat(bits, P_SIZE, axis=0), P_SIZE, axis=1).reshape(LY * LZ)
    frozen = site_bit == bits_lat[None, None, :]
    frozen_in = jnp.where(frozen, u, 0.0).astype(jnp.bfloat16)

    packed = frozen_in[0::2] + frozen_in[1::2]
    tokens = (
        packed.reshape(2, P_SIZE, n_y, P_SIZE, n_z, P_SIZE)
        .transpose(2, 4, 0, 1, 3, 5)
        .reshape(tokens_dev, patch_len // 2)
    )
    bits_f = bits.reshape(1, tokens_dev).astype(jnp.bfloat16)
    send = jnp.concatenate([tokens, bits_f], axis=0)
    gathered, offsets = doubling_gather(send[None], "tm")
    slot_of = np.argsort(np.asarray(offsets)).astype(np.int32)

    w_pair = jnp.concatenate(
        [w_embed[packed_rows(0)], w_embed[packed_rows(1)]], axis=1
    )
    bits_own = bits.reshape(tokens_dev).astype(jnp.float32)
    embedded = embed_packed(tokens, bits_own, w_pair, b_embed)
    normed = layer_norm(embedded, gain_in).astype(jnp.bfloat16)
    queries = jnp.dot(normed, w_qkv[:, :D], preferred_element_type=jnp.float32).astype(
        jnp.bfloat16
    )

    block_rows = lax.dynamic_index_in_dim(block_list, lax.axis_index("tm"), 0, keepdims=False)
    own = lax.axis_index("tm")
    chosen = jnp.take(gathered, jnp.asarray(slot_of)[block_rows ^ own], axis=0)
    n_sel = chosen.shape[0]
    sel_tokens = chosen[:, :tokens_dev, :].reshape(n_sel * tokens_dev, patch_len // 2)
    sel_bits = chosen[:, tokens_dev, :].reshape(n_sel * tokens_dev).astype(jnp.float32)
    sel_embedded = embed_packed(sel_tokens, sel_bits, w_pair, b_embed)
    sel_normed = layer_norm(sel_embedded, gain_in).astype(jnp.bfloat16)
    kv = jnp.dot(sel_normed, w_qkv[:, D:], preferred_element_type=jnp.float32).astype(
        jnp.bfloat16
    )
    keys = kv[:, :D].reshape(n_sel * tokens_dev, HEADS, HS)
    values = kv[:, D:].reshape(n_sel * tokens_dev, HEADS, HS)

    scores = jnp.einsum(
        "qhd,khd->hqk",
        queries.reshape(tokens_dev, HEADS, HS),
        keys,
        preferred_element_type=jnp.float32,
    ) * HS ** (-0.5)
    row_top = jnp.max(scores, axis=-1, keepdims=True)
    exp_scores = jnp.exp(scores - row_top)
    row_total = jnp.sum(exp_scores, axis=-1)
    product = jnp.einsum(
        "hqk,khd->qhd",
        exp_scores.astype(jnp.bfloat16),
        values,
        preferred_element_type=jnp.float32,
    )
    mixed = (product / row_total.T[:, :, None]).reshape(tokens_dev, D)
    hidden = embedded + mixed
    normed_out = layer_norm(hidden, gain_out).astype(jnp.bfloat16)
    tok_ids = lax.broadcasted_iota(jnp.int32, (tokens_dev, LY * LZ), 0)
    lane_ids = lax.broadcasted_iota(jnp.int32, (tokens_dev, LY * LZ), 1)
    tok_lane = tok_ids // n_z * (P_SIZE * LZ) + tok_ids % n_z * P_SIZE
    spread_tok = (lane_ids == tok_lane).astype(jnp.bfloat16)
    normed_lanes = jnp.einsum(
        "tc,tl->cl", normed_out, spread_tok, preferred_element_type=jnp.float32
    ).astype(jnp.bfloat16)
    affine_lanes = jnp.einsum(
        "cj,cl->jl", w_head, normed_lanes, preferred_element_type=jnp.float32
    )
    base_lane = (lane[0, 0] % P_SIZE == 0) & (lane[0, 0] // LZ % P_SIZE == 0)
    affine_lanes = affine_lanes + jnp.where(base_lane[None, :], b_head[:, None], 0.0)
    coupling_rows = jnp.concatenate(
        [jnp.tanh(affine_lanes[:patch_len]), affine_lanes[patch_len:]], axis=0
    ).reshape(2, P_SIZE, P_SIZE, P_SIZE * P_SIZE, LY * LZ)
    coupling_lat = coupling_rows[:, :, :, 0]
    for k in range(1, P_SIZE * P_SIZE):
        offset = k // P_SIZE * LZ + k % P_SIZE
        coupling_lat = coupling_lat + jnp.roll(coupling_rows[:, :, :, k], offset, axis=-1)
    scale_lat = coupling_lat[0]
    shift_lat = coupling_lat[1]
    log_det = jnp.sum(jnp.where(frozen, 0.0, scale_lat))
    new_field = jnp.where(frozen, u, u * jnp.exp(scale_lat) + shift_lat)

    ahead_time = shifted(new_field[0:1].astype(jnp.bfloat16), "tm", -1).astype(jnp.float32)
    ahead_slab = shifted(new_field[:, 0:1].astype(jnp.bfloat16), "space", -1).astype(jnp.float32)
    next_time_field = jnp.concatenate([new_field[1:], ahead_time], axis=0)
    next_slab_field = jnp.concatenate([new_field[:, 1:], ahead_slab], axis=1)
    next_y_field = jnp.roll(new_field, -LZ, axis=2)
    next_z_field = jnp.where(
        lane % LZ == LZ - 1, jnp.roll(new_field, LZ - 1, axis=2), jnp.roll(new_field, -1, axis=2)
    )
    neighbours = next_time_field + next_slab_field
    neighbours = neighbours + next_y_field
    neighbours = neighbours + next_z_field
    squared = new_field * new_field
    density = (
        -2.0 * hopping * new_field * neighbours
        + squared
        + quartic * (squared - 1.0) * (squared - 1.0)
    )
    time_link = new_field * next_time_field
    slab_link = new_field * next_slab_field
    local_log = -0.5 * jnp.sum(u * u) - log_det
    local_act = jnp.sum(density)
    members = lax.axis_size("space") * lax.axis_size("tm")
    partials = jnp.broadcast_to(jnp.stack([local_log, local_act])[None], (members, 2))
    sums = jnp.sum(lax.all_to_all(partials, ("space", "tm"), 0, 0, tiled=True), axis=0)
    sum_log, sum_act = sums[0], sums[1]
    site_count = u.size * lax.axis_size("space") * lax.axis_size("tm")
    totals = jnp.stack([sum_log / site_count - 0.5 * log_two_pi, sum_act / site_count]).astype(
        jnp.float32
    )
    return (new_field, density, time_link, slab_link, totals)


def solution(mesh):
    in_specs = (
        P("tm", "space", None),
        P("tm", "space", None),
        P(),
        P(),
        P(),
        P(),
        P(),
        P(),
        P(),
        P(),
    )
    out_specs = (
        P("tm", "space", None),
        P("tm", "space", None),
        P("tm", "space", None),
        P("tm", "space", None),
        P(),
    )
    return jax.shard_map(shards, mesh=mesh, in_specs=in_specs, out_specs=out_specs, check_vma=False)
```

```python
import math

import numpy as np
import jax
import jax.numpy as jnp
from jax import lax
from jax.sharding import PartitionSpec as P

P_SIZE = 4
D = 768
HEADS = 12
HS = 64
LY = 32
LZ = 64
BLK = 128


hopping = 0.2
quartic = 0.5
epsilon = 1e-05
log_two_pi = math.log(2.0 * math.pi)


def exchange(x, axis, bit):
    length = lax.axis_size(axis)
    return lax.ppermute(x, axis, [(i, i ^ bit) for i in range(length)])


def doubling_sum(x, axis):
    bit = 1
    while bit < lax.axis_size(axis):
        x = x + exchange(x, axis, bit)
        bit *= 2
    return x


def doubling_gather(x, axis):
    bits = []
    bit = 1
    while bit < lax.axis_size(axis):
        bits.append(bit)
        bit *= 2
    offsets = [0]
    for bit in reversed(bits):
        x = jnp.concatenate([x, exchange(x, axis, bit)], axis=0)
        offsets = offsets + [o ^ bit for o in offsets]
    return x, offsets


def shifted(x, axis, by):
    length = lax.axis_size(axis)
    return lax.ppermute(x, axis, [(i, (i + by) % length) for i in range(length)])


def layer_norm(values, gain_vec):
    centre = values - jnp.mean(values, axis=-1, keepdims=True)
    spread = jnp.mean(centre * centre, axis=-1, keepdims=True)
    return centre * lax.rsqrt(spread + epsilon) * gain_vec


def site_parity(patch_side):
    positions = np.arange(patch_side**4, dtype=np.int32)
    return (
        positions // patch_side**3
        + positions // patch_side**2 % patch_side
        + positions // patch_side % patch_side
        + positions % patch_side
    ) % 2


def packed_rows(p_bit):
    th, x4, y4, z4 = np.meshgrid(np.arange(2), np.arange(4), np.arange(4), np.arange(4), indexing="ij")
    t4 = 2 * th + (p_bit + x4 + y4 + z4) % 2
    return (((t4 * 4 + x4) * 4 + y4) * 4 + z4).reshape(-1)


def embed_packed(tokens, bits, w_pair, b_embed):
    both = jnp.dot(tokens, w_pair, preferred_element_type=jnp.float32)
    half = both.shape[-1] // 2
    return jnp.where(bits[..., None] > 0.5, both[..., half:], both[..., :half]) + b_embed


def shards(
    lattice_field, parity, block_list, w_embed, b_embed, gain_in, w_qkv, gain_out, w_head, b_head
):
    n_y = LY // P_SIZE
    n_z = LZ // P_SIZE
    tokens_dev = n_y * n_z
    patch_len = P_SIZE**4
    u = lattice_field
    bits = parity.reshape(n_y, n_z)

    lane = lax.broadcasted_iota(jnp.int32, u.shape, 2)
    t_pos = lax.broadcasted_iota(jnp.int32, u.shape, 0)
    x_pos = lax.broadcasted_iota(jnp.int32, u.shape, 1)
    site_bit = (t_pos + x_pos + lane // LZ + lane % LZ) % 2
    bits_lat = jnp.repeat(jnp.repeat(bits, P_SIZE, axis=0), P_SIZE, axis=1).reshape(LY * LZ)
    frozen = site_bit == bits_lat[None, None, :]
    frozen_in = jnp.where(frozen, u, 0.0).astype(jnp.bfloat16)

    packed = frozen_in[0::2] + frozen_in[1::2]
    tokens = (
        packed.reshape(2, P_SIZE, n_y, P_SIZE, n_z, P_SIZE)
        .transpose(2, 4, 0, 1, 3, 5)
        .reshape(tokens_dev, patch_len // 2)
    )
    bits_f = bits.reshape(1, tokens_dev).astype(jnp.bfloat16)
    send = jnp.concatenate([tokens, bits_f], axis=0)
    gathered, offsets = doubling_gather(send[None], "tm")
    slot_of = np.argsort(np.asarray(offsets)).astype(np.int32)

    w_pair = jnp.concatenate(
        [w_embed[packed_rows(0)], w_embed[packed_rows(1)]], axis=1
    )
    bits_own = bits.reshape(tokens_dev).astype(jnp.float32)
    embedded = embed_packed(tokens, bits_own, w_pair, b_embed)
    normed = layer_norm(embedded, gain_in).astype(jnp.bfloat16)

    block_rows = lax.dynamic_index_in_dim(block_list, lax.axis_index("tm"), 0, keepdims=False)
    own = lax.axis_index("tm")
    chosen = jnp.take(gathered, jnp.asarray(slot_of)[block_rows ^ own], axis=0)
    n_sel = chosen.shape[0]
    sel_tokens = chosen[:, :tokens_dev, :].reshape(n_sel * tokens_dev, patch_len // 2)
    sel_bits = chosen[:, tokens_dev, :].reshape(n_sel * tokens_dev).astype(jnp.float32)
    sel_embedded = embed_packed(sel_tokens, sel_bits, w_pair, b_embed)
    sel_normed = layer_norm(sel_embedded, gain_in).astype(jnp.bfloat16)
    w_heads = w_qkv.reshape(D, 3, HEADS, HS)
    queries = jnp.einsum(
        "tc,chd->htd", normed, w_heads[:, 0], preferred_element_type=jnp.float32
    ).astype(jnp.bfloat16)
    keys_t = jnp.einsum(
        "tc,chd->hdt", sel_normed, w_heads[:, 1], preferred_element_type=jnp.float32
    ).astype(jnp.bfloat16)
    values = jnp.einsum(
        "tc,chd->htd", sel_normed, w_heads[:, 2], preferred_element_type=jnp.float32
    ).astype(jnp.bfloat16)

    scores = jnp.einsum(
        "hqd,hdk->hqk", queries, keys_t, preferred_element_type=jnp.float32
    ) * HS ** (-0.5)
    row_top = jnp.max(scores, axis=-1, keepdims=True)
    exp_scores = jnp.exp(scores - row_top)
    row_total = jnp.sum(exp_scores, axis=-1)
    product = jnp.einsum(
        "hqk,hkd->qhd",
        exp_scores.astype(jnp.bfloat16),
        values,
        preferred_element_type=jnp.float32,
    )
    mixed = (product / row_total.T[:, :, None]).reshape(tokens_dev, D)
    hidden = embedded + mixed
    normed_out = layer_norm(hidden, gain_out).astype(jnp.bfloat16)
    tok_ids = lax.broadcasted_iota(jnp.int32, (tokens_dev, LY * LZ), 0)
    lane_ids = lax.broadcasted_iota(jnp.int32, (tokens_dev, LY * LZ), 1)
    tok_lane = tok_ids // n_z * (P_SIZE * LZ) + tok_ids % n_z * P_SIZE
    spread_tok = (lane_ids == tok_lane).astype(jnp.bfloat16)
    normed_lanes = jnp.einsum(
        "tc,tl->cl", normed_out, spread_tok, preferred_element_type=jnp.float32
    ).astype(jnp.bfloat16)
    n_off = P_SIZE * P_SIZE
    w_rows = w_head.reshape(D, 2 * P_SIZE * P_SIZE, n_off)
    affine_lanes = jnp.einsum(
        "crk,cl->krl", w_rows, normed_lanes, preferred_element_type=jnp.float32
    )
    base_lane = (lane[0, 0] % P_SIZE == 0) & (lane[0, 0] // LZ % P_SIZE == 0)
    bias_rows = b_head.reshape(2 * P_SIZE * P_SIZE, n_off).T
    affine_lanes = affine_lanes + jnp.where(base_lane[None, None, :], bias_rows[:, :, None], 0.0)
    half_rows = P_SIZE * P_SIZE
    coupling_rows = jnp.concatenate(
        [jnp.tanh(affine_lanes[:, :half_rows]), affine_lanes[:, half_rows:]], axis=1
    )
    coupling_lat = coupling_rows[0]
    for k in range(1, n_off):
        offset = k // P_SIZE * LZ + k % P_SIZE
        coupling_lat = coupling_lat + jnp.roll(coupling_rows[k], offset, axis=-1)
    coupling_lat = coupling_lat.reshape(2, P_SIZE, P_SIZE, LY * LZ)
    scale_lat = coupling_lat[0]
    shift_lat = coupling_lat[1]
    log_det = jnp.sum(jnp.where(frozen, 0.0, scale_lat))
    new_field = jnp.where(frozen, u, u * jnp.exp(scale_lat) + shift_lat)

    ahead_time = shifted(new_field[0:1].astype(jnp.bfloat16), "tm", -1).astype(jnp.float32)
    ahead_slab = shifted(new_field[:, 0:1].astype(jnp.bfloat16), "space", -1).astype(jnp.float32)
    next_time_field = jnp.concatenate([new_field[1:], ahead_time], axis=0)
    next_slab_field = jnp.concatenate([new_field[:, 1:], ahead_slab], axis=1)
    next_y_field = jnp.roll(new_field, -LZ, axis=2)
    next_z_field = jnp.where(
        lane % LZ == LZ - 1, jnp.roll(new_field, LZ - 1, axis=2), jnp.roll(new_field, -1, axis=2)
    )
    neighbours = next_time_field + next_slab_field
    neighbours = neighbours + next_y_field
    neighbours = neighbours + next_z_field
    squared = new_field * new_field
    density = (
        -2.0 * hopping * new_field * neighbours
        + squared
        + quartic * (squared - 1.0) * (squared - 1.0)
    )
    time_link = new_field * next_time_field
    slab_link = new_field * next_slab_field
    local_log = -0.5 * jnp.sum(u * u) - log_det
    local_act = jnp.sum(density)
    members = lax.axis_size("space") * lax.axis_size("tm")
    partials = jnp.broadcast_to(jnp.stack([local_log, local_act])[None], (members, 2))
    sums = jnp.sum(lax.all_to_all(partials, ("space", "tm"), 0, 0, tiled=True), axis=0)
    sum_log, sum_act = sums[0], sums[1]
    site_count = u.size * lax.axis_size("space") * lax.axis_size("tm")
    totals = jnp.stack([sum_log / site_count - 0.5 * log_two_pi, sum_act / site_count]).astype(
        jnp.float32
    )
    return (new_field, density, time_link, slab_link, totals)


def solution(mesh):
    in_specs = (
        P("tm", "space", None),
        P("tm", "space", None),
        P(),
        P(),
        P(),
        P(),
        P(),
        P(),
        P(),
        P(),
    )
    out_specs = (
        P("tm", "space", None),
        P("tm", "space", None),
        P("tm", "space", None),
        P("tm", "space", None),
        P(),
    )
    return jax.shard_map(shards, mesh=mesh, in_specs=in_specs, out_specs=out_specs, check_vma=False)
```

```python
import math

import numpy as np
import jax
import jax.numpy as jnp
from jax import lax
from jax.sharding import PartitionSpec as P

P_SIZE = 4
D = 768
HEADS = 12
HS = 64
LY = 32
LZ = 64
BLK = 128


hopping = 0.2
quartic = 0.5
epsilon = 1e-05
log_two_pi = math.log(2.0 * math.pi)


def exchange(x, axis, bit):
    length = lax.axis_size(axis)
    return lax.ppermute(x, axis, [(i, i ^ bit) for i in range(length)])


def doubling_sum(x, axis):
    bit = 1
    while bit < lax.axis_size(axis):
        x = x + exchange(x, axis, bit)
        bit *= 2
    return x


def doubling_gather(x, axis):
    bits = []
    bit = 1
    while bit < lax.axis_size(axis):
        bits.append(bit)
        bit *= 2
    offsets = [0]
    for bit in reversed(bits):
        x = jnp.concatenate([x, exchange(x, axis, bit)], axis=0)
        offsets = offsets + [o ^ bit for o in offsets]
    return x, offsets


def shifted(x, axis, by):
    length = lax.axis_size(axis)
    return lax.ppermute(x, axis, [(i, (i + by) % length) for i in range(length)])


def layer_norm(values, gain_vec):
    centre = values - jnp.mean(values, axis=-1, keepdims=True)
    spread = jnp.mean(centre * centre, axis=-1, keepdims=True)
    return centre * lax.rsqrt(spread + epsilon) * gain_vec


def site_parity(patch_side):
    positions = np.arange(patch_side**4, dtype=np.int32)
    return (
        positions // patch_side**3
        + positions // patch_side**2 % patch_side
        + positions // patch_side % patch_side
        + positions % patch_side
    ) % 2


def packed_rows(p_bit):
    th, x4, y4, z4 = np.meshgrid(np.arange(2), np.arange(4), np.arange(4), np.arange(4), indexing="ij")
    t4 = 2 * th + (p_bit + x4 + y4 + z4) % 2
    return (((t4 * 4 + x4) * 4 + y4) * 4 + z4).reshape(-1)


def embed_packed(tokens, bits, w_pair, b_embed):
    both = jnp.dot(tokens, w_pair, preferred_element_type=jnp.float32)
    half = both.shape[-1] // 2
    return jnp.where(bits[..., None] > 0.5, both[..., half:], both[..., :half]) + b_embed


def shards(
    lattice_field, parity, block_list, w_embed, b_embed, gain_in, w_qkv, gain_out, w_head, b_head
):
    n_y = LY // P_SIZE
    n_z = LZ // P_SIZE
    tokens_dev = n_y * n_z
    patch_len = P_SIZE**4
    u = lattice_field
    bits = parity.reshape(n_y, n_z)

    lane = lax.broadcasted_iota(jnp.int32, u.shape, 2)
    t_pos = lax.broadcasted_iota(jnp.int32, u.shape, 0)
    x_pos = lax.broadcasted_iota(jnp.int32, u.shape, 1)
    site_bit = (t_pos + x_pos + lane // LZ + lane % LZ) % 2
    bits_lat = jnp.repeat(jnp.repeat(bits, P_SIZE, axis=0), P_SIZE, axis=1).reshape(LY * LZ)
    frozen = site_bit == bits_lat[None, None, :]
    frozen_in = jnp.where(frozen, u, 0.0).astype(jnp.bfloat16)

    packed = frozen_in[0::2] + frozen_in[1::2]
    tokens = (
        packed.reshape(2, P_SIZE, n_y, P_SIZE, n_z, P_SIZE)
        .transpose(2, 4, 0, 1, 3, 5)
        .reshape(tokens_dev, patch_len // 2)
    )
    bits_f = bits.reshape(1, tokens_dev).astype(jnp.bfloat16)
    send = jnp.concatenate([tokens, bits_f], axis=0)
    gathered, offsets = doubling_gather(send[None], "tm")
    slot_of = np.argsort(np.asarray(offsets)).astype(np.int32)

    w_pair = jnp.concatenate(
        [w_embed[packed_rows(0)], w_embed[packed_rows(1)]], axis=1
    )
    bits_own = bits.reshape(tokens_dev).astype(jnp.float32)
    embedded = embed_packed(tokens, bits_own, w_pair, b_embed)
    normed = layer_norm(embedded, gain_in).astype(jnp.bfloat16)

    block_rows = lax.dynamic_index_in_dim(block_list, lax.axis_index("tm"), 0, keepdims=False)
    own = lax.axis_index("tm")
    chosen = jnp.take(gathered, jnp.asarray(slot_of)[block_rows ^ own], axis=0)
    n_sel = chosen.shape[0]
    sel_tokens = chosen[:, :tokens_dev, :].reshape(n_sel * tokens_dev, patch_len // 2)
    sel_bits = chosen[:, tokens_dev, :].reshape(n_sel * tokens_dev).astype(jnp.float32)
    sel_embedded = embed_packed(sel_tokens, sel_bits, w_pair, b_embed)
    sel_normed = layer_norm(sel_embedded, gain_in).astype(jnp.bfloat16)
    queries = jnp.dot(normed, w_qkv[:, :D], preferred_element_type=jnp.float32).astype(
        jnp.bfloat16
    )
    kv = jnp.dot(sel_normed, w_qkv[:, D:], preferred_element_type=jnp.float32).astype(
        jnp.bfloat16
    )
    keys = kv[:, :D].reshape(n_sel * tokens_dev, HEADS, HS)
    values = kv[:, D:].reshape(n_sel * tokens_dev, HEADS, HS)

    scores = jnp.einsum(
        "qhd,khd->hqk",
        queries.reshape(tokens_dev, HEADS, HS),
        keys,
        preferred_element_type=jnp.float32,
    ) * HS ** (-0.5)
    row_top = jnp.max(scores, axis=-1, keepdims=True)
    exp_scores = jnp.exp(scores - row_top)
    row_total = jnp.sum(exp_scores, axis=-1)
    product = jnp.einsum(
        "hqk,khd->qhd",
        exp_scores.astype(jnp.bfloat16),
        values,
        preferred_element_type=jnp.float32,
    )
    mixed = (product / row_total.T[:, :, None]).reshape(tokens_dev, D)
    hidden = embedded + mixed
    normed_out = layer_norm(hidden, gain_out).astype(jnp.bfloat16)
    tok_ids = lax.broadcasted_iota(jnp.int32, (tokens_dev, LY * LZ), 0)
    lane_ids = lax.broadcasted_iota(jnp.int32, (tokens_dev, LY * LZ), 1)
    tok_lane = tok_ids // n_z * (P_SIZE * LZ) + tok_ids % n_z * P_SIZE
    spread_tok = (lane_ids == tok_lane).astype(jnp.bfloat16)
    normed_lanes = jnp.einsum(
        "tc,tl->cl", normed_out, spread_tok, preferred_element_type=jnp.float32
    ).astype(jnp.bfloat16)
    n_off = P_SIZE * P_SIZE
    w_rows = w_head.reshape(D, 2 * P_SIZE * P_SIZE, n_off)
    affine_lanes = jnp.einsum(
        "crk,cl->krl", w_rows, normed_lanes, preferred_element_type=jnp.float32
    )
    base_lane = (lane[0, 0] % P_SIZE == 0) & (lane[0, 0] // LZ % P_SIZE == 0)
    bias_rows = b_head.reshape(2 * P_SIZE * P_SIZE, n_off).T
    affine_lanes = affine_lanes + jnp.where(base_lane[None, None, :], bias_rows[:, :, None], 0.0)
    half_rows = P_SIZE * P_SIZE
    coupling_rows = jnp.concatenate(
        [jnp.tanh(affine_lanes[:, :half_rows]), affine_lanes[:, half_rows:]], axis=1
    )
    coupling_lat = coupling_rows[0]
    for k in range(1, n_off):
        offset = k // P_SIZE * LZ + k % P_SIZE
        coupling_lat = coupling_lat + jnp.roll(coupling_rows[k], offset, axis=-1)
    coupling_lat = coupling_lat.reshape(2, P_SIZE, P_SIZE, LY * LZ)
    scale_lat = coupling_lat[0]
    shift_lat = coupling_lat[1]
    log_det = jnp.sum(jnp.where(frozen, 0.0, scale_lat))
    new_field = jnp.where(frozen, u, u * jnp.exp(scale_lat) + shift_lat)

    ahead_time = shifted(new_field[0:1].astype(jnp.bfloat16), "tm", -1).astype(jnp.float32)
    ahead_slab = shifted(new_field[:, 0:1].astype(jnp.bfloat16), "space", -1).astype(jnp.float32)
    next_time_field = jnp.concatenate([new_field[1:], ahead_time], axis=0)
    next_slab_field = jnp.concatenate([new_field[:, 1:], ahead_slab], axis=1)
    next_y_field = jnp.roll(new_field, -LZ, axis=2)
    next_z_field = jnp.where(
        lane % LZ == LZ - 1, jnp.roll(new_field, LZ - 1, axis=2), jnp.roll(new_field, -1, axis=2)
    )
    neighbours = next_time_field + next_slab_field
    neighbours = neighbours + next_y_field
    neighbours = neighbours + next_z_field
    squared = new_field * new_field
    density = (
        -2.0 * hopping * new_field * neighbours
        + squared
        + quartic * (squared - 1.0) * (squared - 1.0)
    )
    time_link = new_field * next_time_field
    slab_link = new_field * next_slab_field
    local_log = -0.5 * jnp.sum(u * u) - log_det
    local_act = jnp.sum(density)
    members = lax.axis_size("space") * lax.axis_size("tm")
    partials = jnp.broadcast_to(jnp.stack([local_log, local_act])[None], (members, 2))
    sums = jnp.sum(lax.all_to_all(partials, ("space", "tm"), 0, 0, tiled=True), axis=0)
    sum_log, sum_act = sums[0], sums[1]
    site_count = u.size * lax.axis_size("space") * lax.axis_size("tm")
    totals = jnp.stack([sum_log / site_count - 0.5 * log_two_pi, sum_act / site_count]).astype(
        jnp.float32
    )
    return (new_field, density, time_link, slab_link, totals)


def solution(mesh):
    in_specs = (
        P("tm", "space", None),
        P("tm", "space", None),
        P(),
        P(),
        P(),
        P(),
        P(),
        P(),
        P(),
        P(),
    )
    out_specs = (
        P("tm", "space", None),
        P("tm", "space", None),
        P("tm", "space", None),
        P("tm", "space", None),
        P(),
    )
    return jax.shard_map(shards, mesh=mesh, in_specs=in_specs, out_specs=out_specs, check_vma=False)
```

```python
import math

import numpy as np
import jax
import jax.numpy as jnp
from jax import lax
from jax.sharding import PartitionSpec as P

P_SIZE = 4
D = 768
HEADS = 12
HS = 64
LY = 32
LZ = 64
BLK = 128


hopping = 0.2
quartic = 0.5
epsilon = 1e-05
log_two_pi = math.log(2.0 * math.pi)


def exchange(x, axis, bit):
    length = lax.axis_size(axis)
    return lax.ppermute(x, axis, [(i, i ^ bit) for i in range(length)])


def doubling_sum(x, axis):
    bit = 1
    while bit < lax.axis_size(axis):
        x = x + exchange(x, axis, bit)
        bit *= 2
    return x


def doubling_gather(x, axis):
    bits = []
    bit = 1
    while bit < lax.axis_size(axis):
        bits.append(bit)
        bit *= 2
    offsets = [0]
    for bit in reversed(bits):
        x = jnp.concatenate([x, exchange(x, axis, bit)], axis=0)
        offsets = offsets + [o ^ bit for o in offsets]
    return x, offsets


def shifted(x, axis, by):
    length = lax.axis_size(axis)
    return lax.ppermute(x, axis, [(i, (i + by) % length) for i in range(length)])


def layer_norm(values, gain_vec):
    centre = values - jnp.mean(values, axis=-1, keepdims=True)
    spread = jnp.mean(centre * centre, axis=-1, keepdims=True)
    return centre * lax.rsqrt(spread + epsilon) * gain_vec


def site_parity(patch_side):
    positions = np.arange(patch_side**4, dtype=np.int32)
    return (
        positions // patch_side**3
        + positions // patch_side**2 % patch_side
        + positions // patch_side % patch_side
        + positions % patch_side
    ) % 2


def packed_rows(p_bit):
    th, x4, y4, z4 = np.meshgrid(np.arange(2), np.arange(4), np.arange(4), np.arange(4), indexing="ij")
    t4 = 2 * th + (p_bit + x4 + y4 + z4) % 2
    return (((t4 * 4 + x4) * 4 + y4) * 4 + z4).reshape(-1)


def embed_packed(tokens, bits, w_pair, b_embed):
    both = jnp.dot(tokens, w_pair, preferred_element_type=jnp.float32)
    half = both.shape[-1] // 2
    return jnp.where(bits[..., None] > 0.5, both[..., half:], both[..., :half]) + b_embed


def shards(
    lattice_field, parity, block_list, w_embed, b_embed, gain_in, w_qkv, gain_out, w_head, b_head
):
    n_y = LY // P_SIZE
    n_z = LZ // P_SIZE
    tokens_dev = n_y * n_z
    patch_len = P_SIZE**4
    u = lattice_field
    bits = parity.reshape(n_y, n_z)

    lane = lax.broadcasted_iota(jnp.int32, u.shape, 2)
    t_pos = lax.broadcasted_iota(jnp.int32, u.shape, 0)
    x_pos = lax.broadcasted_iota(jnp.int32, u.shape, 1)
    site_bit = (t_pos + x_pos + lane // LZ + lane % LZ) % 2
    bits_lat = jnp.repeat(jnp.repeat(bits, P_SIZE, axis=0), P_SIZE, axis=1).reshape(LY * LZ)
    frozen = site_bit == bits_lat[None, None, :]
    frozen_in = jnp.where(frozen, u, 0.0).astype(jnp.bfloat16)

    packed = frozen_in[0::2] + frozen_in[1::2]
    n_off = P_SIZE * P_SIZE
    tok_ids = lax.broadcasted_iota(jnp.int32, (tokens_dev, LY * LZ), 0)
    lane_ids = lax.broadcasted_iota(jnp.int32, (tokens_dev, LY * LZ), 1)
    tok_lane = tok_ids // n_z * (P_SIZE * LZ) + tok_ids % n_z * P_SIZE
    spread_tok = (lane_ids == tok_lane).astype(jnp.bfloat16)
    packed_rows_lat = packed.reshape(2 * P_SIZE, LY * LZ)
    shifted_rows = jnp.stack(
        [
            jnp.roll(packed_rows_lat, -(k // P_SIZE * LZ + k % P_SIZE), axis=-1)
            for k in range(n_off)
        ],
        axis=1,
    ).reshape(2 * P_SIZE * n_off, LY * LZ)
    tokens = jnp.einsum(
        "fl,tl->tf", shifted_rows, spread_tok, preferred_element_type=jnp.float32
    ).astype(jnp.bfloat16)
    bits_f = bits.reshape(1, tokens_dev).astype(jnp.bfloat16)
    send = jnp.concatenate([tokens, bits_f], axis=0)
    gathered, offsets = doubling_gather(send[None], "tm")
    slot_of = np.argsort(np.asarray(offsets)).astype(np.int32)

    w_pair = jnp.concatenate(
        [w_embed[packed_rows(0)], w_embed[packed_rows(1)]], axis=1
    )
    bits_own = bits.reshape(tokens_dev).astype(jnp.float32)
    embedded = embed_packed(tokens, bits_own, w_pair, b_embed)
    normed = layer_norm(embedded, gain_in).astype(jnp.bfloat16)

    block_rows = lax.dynamic_index_in_dim(block_list, lax.axis_index("tm"), 0, keepdims=False)
    own = lax.axis_index("tm")
    chosen = jnp.take(gathered, jnp.asarray(slot_of)[block_rows ^ own], axis=0)
    n_sel = chosen.shape[0]
    sel_tokens = chosen[:, :tokens_dev, :].reshape(n_sel * tokens_dev, patch_len // 2)
    sel_bits = chosen[:, tokens_dev, :].reshape(n_sel * tokens_dev).astype(jnp.float32)
    sel_embedded = embed_packed(sel_tokens, sel_bits, w_pair, b_embed)
    sel_normed = layer_norm(sel_embedded, gain_in).astype(jnp.bfloat16)
    queries = jnp.dot(normed, w_qkv[:, :D], preferred_element_type=jnp.float32).astype(
        jnp.bfloat16
    )
    kv = jnp.dot(sel_normed, w_qkv[:, D:], preferred_element_type=jnp.float32).astype(
        jnp.bfloat16
    )
    keys = kv[:, :D].reshape(n_sel * tokens_dev, HEADS, HS)
    values = kv[:, D:].reshape(n_sel * tokens_dev, HEADS, HS)

    scores = jnp.einsum(
        "qhd,khd->hqk",
        queries.reshape(tokens_dev, HEADS, HS),
        keys,
        preferred_element_type=jnp.float32,
    ) * HS ** (-0.5)
    row_top = jnp.max(scores, axis=-1, keepdims=True)
    exp_scores = jnp.exp(scores - row_top)
    row_total = jnp.sum(exp_scores, axis=-1)
    product = jnp.einsum(
        "hqk,khd->qhd",
        exp_scores.astype(jnp.bfloat16),
        values,
        preferred_element_type=jnp.float32,
    )
    mixed = (product / row_total.T[:, :, None]).reshape(tokens_dev, D)
    hidden = embedded + mixed
    normed_out = layer_norm(hidden, gain_out).astype(jnp.bfloat16)
    normed_lanes = jnp.einsum(
        "tc,tl->cl", normed_out, spread_tok, preferred_element_type=jnp.float32
    ).astype(jnp.bfloat16)
    w_rows = w_head.reshape(D, 2 * P_SIZE * P_SIZE, n_off)
    affine_lanes = jnp.einsum(
        "crk,cl->krl", w_rows, normed_lanes, preferred_element_type=jnp.float32
    )
    base_lane = (lane[0, 0] % P_SIZE == 0) & (lane[0, 0] // LZ % P_SIZE == 0)
    bias_rows = b_head.reshape(2 * P_SIZE * P_SIZE, n_off).T
    affine_lanes = affine_lanes + jnp.where(base_lane[None, None, :], bias_rows[:, :, None], 0.0)
    coupling_lat = affine_lanes[0]
    for k in range(1, n_off):
        offset = k // P_SIZE * LZ + k % P_SIZE
        coupling_lat = coupling_lat + jnp.roll(affine_lanes[k], offset, axis=-1)
    half_rows = P_SIZE * P_SIZE
    scale_lat = jnp.tanh(coupling_lat[:half_rows]).reshape(P_SIZE, P_SIZE, LY * LZ)
    shift_lat = coupling_lat[half_rows:].reshape(P_SIZE, P_SIZE, LY * LZ)
    log_det = jnp.sum(jnp.where(frozen, 0.0, scale_lat))
    new_field = jnp.where(frozen, u, u * jnp.exp(scale_lat) + shift_lat)

    ahead_time = shifted(new_field[0:1].astype(jnp.bfloat16), "tm", -1).astype(jnp.float32)
    ahead_slab = shifted(new_field[:, 0:1].astype(jnp.bfloat16), "space", -1).astype(jnp.float32)
    next_time_field = jnp.concatenate([new_field[1:], ahead_time], axis=0)
    next_slab_field = jnp.concatenate([new_field[:, 1:], ahead_slab], axis=1)
    next_y_field = jnp.roll(new_field, -LZ, axis=2)
    next_z_field = jnp.where(
        lane % LZ == LZ - 1, jnp.roll(new_field, LZ - 1, axis=2), jnp.roll(new_field, -1, axis=2)
    )
    neighbours = next_time_field + next_slab_field
    neighbours = neighbours + next_y_field
    neighbours = neighbours + next_z_field
    squared = new_field * new_field
    density = (
        -2.0 * hopping * new_field * neighbours
        + squared
        + quartic * (squared - 1.0) * (squared - 1.0)
    )
    time_link = new_field * next_time_field
    slab_link = new_field * next_slab_field
    local_log = -0.5 * jnp.sum(u * u) - log_det
    local_act = jnp.sum(density)
    members = lax.axis_size("space") * lax.axis_size("tm")
    partials = jnp.broadcast_to(jnp.stack([local_log, local_act])[None], (members, 2))
    sums = jnp.sum(lax.all_to_all(partials, ("space", "tm"), 0, 0, tiled=True), axis=0)
    sum_log, sum_act = sums[0], sums[1]
    site_count = u.size * lax.axis_size("space") * lax.axis_size("tm")
    totals = jnp.stack([sum_log / site_count - 0.5 * log_two_pi, sum_act / site_count]).astype(
        jnp.float32
    )
    return (new_field, density, time_link, slab_link, totals)


def solution(mesh):
    in_specs = (
        P("tm", "space", None),
        P("tm", "space", None),
        P(),
        P(),
        P(),
        P(),
        P(),
        P(),
        P(),
        P(),
    )
    out_specs = (
        P("tm", "space", None),
        P("tm", "space", None),
        P("tm", "space", None),
        P("tm", "space", None),
        P(),
    )
    return jax.shard_map(shards, mesh=mesh, in_specs=in_specs, out_specs=out_specs, check_vma=False)
```

```python
import math

import numpy as np
import jax
import jax.numpy as jnp
from jax import lax
from jax.sharding import PartitionSpec as P

P_SIZE = 4
D = 768
HEADS = 12
HS = 64
LY = 32
LZ = 64
BLK = 128


hopping = 0.2
quartic = 0.5
epsilon = 1e-05
log_two_pi = math.log(2.0 * math.pi)


def exchange(x, axis, bit):
    length = lax.axis_size(axis)
    return lax.ppermute(x, axis, [(i, i ^ bit) for i in range(length)])


def doubling_sum(x, axis):
    bit = 1
    while bit < lax.axis_size(axis):
        x = x + exchange(x, axis, bit)
        bit *= 2
    return x


def doubling_gather(x, axis):
    bits = []
    bit = 1
    while bit < lax.axis_size(axis):
        bits.append(bit)
        bit *= 2
    offsets = [0]
    for bit in reversed(bits):
        x = jnp.concatenate([x, exchange(x, axis, bit)], axis=0)
        offsets = offsets + [o ^ bit for o in offsets]
    return x, offsets


def shifted(x, axis, by):
    length = lax.axis_size(axis)
    return lax.ppermute(x, axis, [(i, (i + by) % length) for i in range(length)])


def layer_norm(values, gain_vec):
    centre = values - jnp.mean(values, axis=-1, keepdims=True)
    spread = jnp.mean(centre * centre, axis=-1, keepdims=True)
    return centre * lax.rsqrt(spread + epsilon) * gain_vec


def site_parity(patch_side):
    positions = np.arange(patch_side**4, dtype=np.int32)
    return (
        positions // patch_side**3
        + positions // patch_side**2 % patch_side
        + positions // patch_side % patch_side
        + positions % patch_side
    ) % 2


def packed_rows(p_bit):
    th, x4, y4, z4 = np.meshgrid(np.arange(2), np.arange(4), np.arange(4), np.arange(4), indexing="ij")
    t4 = 2 * th + (p_bit + x4 + y4 + z4) % 2
    return (((t4 * 4 + x4) * 4 + y4) * 4 + z4).reshape(-1)


def embed_packed(tokens, bits, w_pair, b_embed):
    both = jnp.dot(tokens, w_pair, preferred_element_type=jnp.float32)
    half = both.shape[-1] // 2
    return jnp.where(bits[..., None] > 0.5, both[..., half:], both[..., :half]) + b_embed


def shards(
    lattice_field, parity, block_list, w_embed, b_embed, gain_in, w_qkv, gain_out, w_head, b_head
):
    n_y = LY // P_SIZE
    n_z = LZ // P_SIZE
    tokens_dev = n_y * n_z
    patch_len = P_SIZE**4
    u = lattice_field
    bits = parity.reshape(n_y, n_z)

    lane = lax.broadcasted_iota(jnp.int32, u.shape, 2)
    t_pos = lax.broadcasted_iota(jnp.int32, u.shape, 0)
    x_pos = lax.broadcasted_iota(jnp.int32, u.shape, 1)
    site_bit = (t_pos + x_pos + lane // LZ + lane % LZ) % 2
    bits_lat = jnp.repeat(jnp.repeat(bits, P_SIZE, axis=0), P_SIZE, axis=1).reshape(LY * LZ)
    frozen = site_bit == bits_lat[None, None, :]
    frozen_in = jnp.where(frozen, u, 0.0).astype(jnp.bfloat16)

    packed = frozen_in[0::2] + frozen_in[1::2]
    n_off = P_SIZE * P_SIZE
    tok_ids = lax.broadcasted_iota(jnp.int32, (tokens_dev, LY * LZ), 0)
    lane_ids = lax.broadcasted_iota(jnp.int32, (tokens_dev, LY * LZ), 1)
    tok_lane = tok_ids // n_z * (P_SIZE * LZ) + tok_ids % n_z * P_SIZE
    spread_tok = (lane_ids == tok_lane).astype(jnp.bfloat16)
    packed_rows_lat = packed.reshape(2 * P_SIZE, LY * LZ)
    shifted_rows = jnp.stack(
        [
            jnp.roll(packed_rows_lat, -(k // P_SIZE * LZ + k % P_SIZE), axis=-1)
            for k in range(n_off)
        ],
        axis=1,
    ).reshape(2 * P_SIZE * n_off, LY * LZ)
    tokens = jnp.einsum(
        "fl,tl->tf", shifted_rows, spread_tok, preferred_element_type=jnp.float32
    ).astype(jnp.bfloat16)
    bits_f = bits.reshape(1, tokens_dev).astype(jnp.bfloat16)
    send = jnp.concatenate([tokens, bits_f], axis=0)
    gathered, offsets = doubling_gather(send[None], "tm")
    slot_of = np.argsort(np.asarray(offsets)).astype(np.int32)

    w_pair = jnp.concatenate(
        [w_embed[packed_rows(0)], w_embed[packed_rows(1)]], axis=1
    )
    bits_own = bits.reshape(tokens_dev).astype(jnp.float32)
    embedded = embed_packed(tokens, bits_own, w_pair, b_embed)
    normed = layer_norm(embedded, gain_in).astype(jnp.bfloat16)

    block_rows = lax.dynamic_index_in_dim(block_list, lax.axis_index("tm"), 0, keepdims=False)
    own = lax.axis_index("tm")
    chosen = jnp.take(gathered, jnp.asarray(slot_of)[block_rows ^ own], axis=0)
    n_sel = chosen.shape[0]
    sel_tokens = chosen[:, :tokens_dev, :].reshape(n_sel * tokens_dev, patch_len // 2)
    sel_bits = chosen[:, tokens_dev, :].reshape(n_sel * tokens_dev).astype(jnp.float32)
    sel_embedded = embed_packed(sel_tokens, sel_bits, w_pair, b_embed)
    sel_normed = layer_norm(sel_embedded, gain_in).astype(jnp.bfloat16)
    queries = jnp.dot(normed, w_qkv[:, :D], preferred_element_type=jnp.float32).astype(
        jnp.bfloat16
    )
    kv = jnp.dot(sel_normed, w_qkv[:, D:], preferred_element_type=jnp.float32).astype(
        jnp.bfloat16
    )
    keys = kv[:, :D].reshape(n_sel * tokens_dev, HEADS, HS)
    values = kv[:, D:].reshape(n_sel * tokens_dev, HEADS, HS)

    scores = jnp.einsum(
        "qhd,khd->hqk",
        queries.reshape(tokens_dev, HEADS, HS),
        keys,
        preferred_element_type=jnp.float32,
    ) * HS ** (-0.5)
    row_top = jnp.max(scores, axis=-1, keepdims=True)
    exp_scores = jnp.exp(scores - row_top)
    row_total = jnp.sum(exp_scores, axis=-1)
    product = jnp.einsum(
        "hqk,khd->qhd",
        exp_scores.astype(jnp.bfloat16),
        values,
        preferred_element_type=jnp.float32,
    )
    mixed = (product / row_total.T[:, :, None]).reshape(tokens_dev, D)
    hidden = embedded + mixed
    normed_out = layer_norm(hidden, gain_out).astype(jnp.bfloat16)
    w_rows = w_head.reshape(D, 2 * P_SIZE * P_SIZE, n_off)
    affine_rows = jnp.einsum(
        "tc,crk->krt", normed_out, w_rows, preferred_element_type=jnp.float32
    ) + b_head.reshape(2 * P_SIZE * P_SIZE, n_off).T[:, :, None]
    high = lax.reduce_precision(affine_rows, exponent_bits=8, mantissa_bits=7)
    rest = affine_rows - high
    middle = lax.reduce_precision(rest, exponent_bits=8, mantissa_bits=7)
    low = rest - middle
    pieces = jnp.concatenate([high, middle, low], axis=-1).astype(jnp.bfloat16)
    spread_three = jnp.concatenate([spread_tok, spread_tok, spread_tok], axis=0)
    affine_lanes = jnp.einsum(
        "krt,tl->krl", pieces, spread_three, preferred_element_type=jnp.float32
    )
    coupling_lat = affine_lanes[0]
    for k in range(1, n_off):
        offset = k // P_SIZE * LZ + k % P_SIZE
        coupling_lat = coupling_lat + jnp.roll(affine_lanes[k], offset, axis=-1)
    half_rows = P_SIZE * P_SIZE
    scale_lat = jnp.tanh(coupling_lat[:half_rows]).reshape(P_SIZE, P_SIZE, LY * LZ)
    shift_lat = coupling_lat[half_rows:].reshape(P_SIZE, P_SIZE, LY * LZ)
    log_det = jnp.sum(jnp.where(frozen, 0.0, scale_lat))
    new_field = jnp.where(frozen, u, u * jnp.exp(scale_lat) + shift_lat)

    ahead_time = shifted(new_field[0:1].astype(jnp.bfloat16), "tm", -1).astype(jnp.float32)
    ahead_slab = shifted(new_field[:, 0:1].astype(jnp.bfloat16), "space", -1).astype(jnp.float32)
    next_time_field = jnp.concatenate([new_field[1:], ahead_time], axis=0)
    next_slab_field = jnp.concatenate([new_field[:, 1:], ahead_slab], axis=1)
    next_y_field = jnp.roll(new_field, -LZ, axis=2)
    next_z_field = jnp.where(
        lane % LZ == LZ - 1, jnp.roll(new_field, LZ - 1, axis=2), jnp.roll(new_field, -1, axis=2)
    )
    neighbours = next_time_field + next_slab_field
    neighbours = neighbours + next_y_field
    neighbours = neighbours + next_z_field
    squared = new_field * new_field
    density = (
        -2.0 * hopping * new_field * neighbours
        + squared
        + quartic * (squared - 1.0) * (squared - 1.0)
    )
    time_link = new_field * next_time_field
    slab_link = new_field * next_slab_field
    local_log = -0.5 * jnp.sum(u * u) - log_det
    local_act = jnp.sum(density)
    members = lax.axis_size("space") * lax.axis_size("tm")
    partials = jnp.broadcast_to(jnp.stack([local_log, local_act])[None], (members, 2))
    sums = jnp.sum(lax.all_to_all(partials, ("space", "tm"), 0, 0, tiled=True), axis=0)
    sum_log, sum_act = sums[0], sums[1]
    site_count = u.size * lax.axis_size("space") * lax.axis_size("tm")
    totals = jnp.stack([sum_log / site_count - 0.5 * log_two_pi, sum_act / site_count]).astype(
        jnp.float32
    )
    return (new_field, density, time_link, slab_link, totals)


def solution(mesh):
    in_specs = (
        P("tm", "space", None),
        P("tm", "space", None),
        P(),
        P(),
        P(),
        P(),
        P(),
        P(),
        P(),
        P(),
    )
    out_specs = (
        P("tm", "space", None),
        P("tm", "space", None),
        P("tm", "space", None),
        P("tm", "space", None),
        P(),
    )
    return jax.shard_map(shards, mesh=mesh, in_specs=in_specs, out_specs=out_specs, check_vma=False)
```

```python
import math

import numpy as np
import jax
import jax.numpy as jnp
from jax import lax
from jax.sharding import PartitionSpec as P

P_SIZE = 4
D = 768
HEADS = 12
HS = 64
LY = 32
LZ = 64
BLK = 128


hopping = 0.2
quartic = 0.5
epsilon = 1e-05
log_two_pi = math.log(2.0 * math.pi)


def exchange(x, axis, bit):
    length = lax.axis_size(axis)
    return lax.ppermute(x, axis, [(i, i ^ bit) for i in range(length)])


def doubling_sum(x, axis):
    bit = 1
    while bit < lax.axis_size(axis):
        x = x + exchange(x, axis, bit)
        bit *= 2
    return x


def doubling_gather(x, axis):
    bits = []
    bit = 1
    while bit < lax.axis_size(axis):
        bits.append(bit)
        bit *= 2
    offsets = [0]
    for bit in reversed(bits):
        x = jnp.concatenate([x, exchange(x, axis, bit)], axis=0)
        offsets = offsets + [o ^ bit for o in offsets]
    return x, offsets


def shifted(x, axis, by):
    length = lax.axis_size(axis)
    return lax.ppermute(x, axis, [(i, (i + by) % length) for i in range(length)])


def layer_norm(values, gain_vec):
    centre = values - jnp.mean(values, axis=-1, keepdims=True)
    spread = jnp.mean(centre * centre, axis=-1, keepdims=True)
    return centre * lax.rsqrt(spread + epsilon) * gain_vec


def site_parity(patch_side):
    positions = np.arange(patch_side**4, dtype=np.int32)
    return (
        positions // patch_side**3
        + positions // patch_side**2 % patch_side
        + positions // patch_side % patch_side
        + positions % patch_side
    ) % 2


def packed_rows(p_bit):
    th, x4, y4, z4 = np.meshgrid(np.arange(2), np.arange(4), np.arange(4), np.arange(4), indexing="ij")
    t4 = 2 * th + (p_bit + x4 + y4 + z4) % 2
    return (((t4 * 4 + x4) * 4 + y4) * 4 + z4).reshape(-1)


def embed_packed(tokens, bits, w_pair, b_embed):
    both = jnp.dot(tokens, w_pair, preferred_element_type=jnp.float32)
    half = both.shape[-1] // 2
    return jnp.where(bits[..., None] > 0.5, both[..., half:], both[..., :half]) + b_embed


def shards(
    lattice_field, parity, block_list, w_embed, b_embed, gain_in, w_qkv, gain_out, w_head, b_head
):
    n_y = LY // P_SIZE
    n_z = LZ // P_SIZE
    tokens_dev = n_y * n_z
    patch_len = P_SIZE**4
    u = lattice_field
    bits = parity.reshape(n_y, n_z)

    lane = lax.broadcasted_iota(jnp.int32, u.shape, 2)
    t_pos = lax.broadcasted_iota(jnp.int32, u.shape, 0)
    x_pos = lax.broadcasted_iota(jnp.int32, u.shape, 1)
    site_bit = (t_pos + x_pos + lane // LZ + lane % LZ) % 2
    bits_lat = jnp.repeat(jnp.repeat(bits, P_SIZE, axis=0), P_SIZE, axis=1).reshape(LY * LZ)
    frozen = site_bit == bits_lat[None, None, :]
    frozen_in = jnp.where(frozen, u, 0.0).astype(jnp.bfloat16)

    packed = frozen_in[0::2] + frozen_in[1::2]
    n_off = P_SIZE * P_SIZE
    tok_ids = lax.broadcasted_iota(jnp.int32, (tokens_dev, LY * LZ), 0)
    lane_ids = lax.broadcasted_iota(jnp.int32, (tokens_dev, LY * LZ), 1)
    tok_lane = tok_ids // n_z * (P_SIZE * LZ) + tok_ids % n_z * P_SIZE
    spread_tok = (lane_ids == tok_lane).astype(jnp.bfloat16)
    packed_rows_lat = packed.reshape(2 * P_SIZE, LY * LZ)
    shifted_rows = jnp.stack(
        [
            jnp.roll(packed_rows_lat, -(k // P_SIZE * LZ + k % P_SIZE), axis=-1)
            for k in range(n_off)
        ],
        axis=1,
    ).reshape(2 * P_SIZE * n_off, LY * LZ)
    tokens = jnp.einsum(
        "fl,tl->tf", shifted_rows, spread_tok, preferred_element_type=jnp.float32
    ).astype(jnp.bfloat16)
    bits_f = bits.reshape(1, tokens_dev).astype(jnp.bfloat16)
    send = jnp.concatenate([tokens, bits_f], axis=0)
    gathered, offsets = doubling_gather(send[None], "tm")
    slot_of = np.argsort(np.asarray(offsets)).astype(np.int32)

    w_pair = jnp.concatenate(
        [w_embed[packed_rows(0)], w_embed[packed_rows(1)]], axis=1
    )
    bits_own = bits.reshape(tokens_dev).astype(jnp.float32)
    embedded = embed_packed(tokens, bits_own, w_pair, b_embed)
    normed = layer_norm(embedded, gain_in).astype(jnp.bfloat16)

    block_rows = lax.dynamic_index_in_dim(block_list, lax.axis_index("tm"), 0, keepdims=False)
    own = lax.axis_index("tm")
    chosen = jnp.take(gathered, jnp.asarray(slot_of)[block_rows ^ own], axis=0)
    n_sel = chosen.shape[0]
    sel_tokens = chosen[:, :tokens_dev, :].reshape(n_sel * tokens_dev, patch_len // 2)
    sel_bits = chosen[:, tokens_dev, :].reshape(n_sel * tokens_dev).astype(jnp.float32)
    sel_embedded = embed_packed(sel_tokens, sel_bits, w_pair, b_embed)
    sel_normed = layer_norm(sel_embedded, gain_in).astype(jnp.bfloat16)
    queries = jnp.dot(normed, w_qkv[:, :D], preferred_element_type=jnp.float32).astype(
        jnp.bfloat16
    )
    w_kv = w_qkv[:, D:].reshape(D, 2, HEADS, HS)
    kv = jnp.einsum(
        "tc,cnhd->nhtd", sel_normed, w_kv, preferred_element_type=jnp.float32
    ).astype(jnp.bfloat16)
    keys = kv[0]
    values = kv[1]

    scores = jnp.einsum(
        "qhd,hkd->hqk",
        queries.reshape(tokens_dev, HEADS, HS),
        keys,
        preferred_element_type=jnp.float32,
    ) * HS ** (-0.5)
    row_top = jnp.max(scores, axis=-1, keepdims=True)
    exp_scores = jnp.exp(scores - row_top)
    row_total = jnp.sum(exp_scores, axis=-1)
    product = jnp.einsum(
        "hqk,hkd->qhd",
        exp_scores.astype(jnp.bfloat16),
        values,
        preferred_element_type=jnp.float32,
    )
    mixed = (product / row_total.T[:, :, None]).reshape(tokens_dev, D)
    hidden = embedded + mixed
    normed_out = layer_norm(hidden, gain_out).astype(jnp.bfloat16)
    w_rows = w_head.reshape(D, 2 * P_SIZE * P_SIZE, n_off)
    affine_rows = jnp.einsum(
        "tc,crk->krt", normed_out, w_rows, preferred_element_type=jnp.float32
    ) + b_head.reshape(2 * P_SIZE * P_SIZE, n_off).T[:, :, None]
    high = lax.reduce_precision(affine_rows, exponent_bits=8, mantissa_bits=7)
    rest = affine_rows - high
    middle = lax.reduce_precision(rest, exponent_bits=8, mantissa_bits=7)
    low = rest - middle
    pieces = jnp.concatenate([high, middle, low], axis=-1).astype(jnp.bfloat16)
    spread_three = jnp.concatenate([spread_tok, spread_tok, spread_tok], axis=0)
    affine_lanes = jnp.einsum(
        "krt,tl->krl", pieces, spread_three, preferred_element_type=jnp.float32
    )
    coupling_lat = affine_lanes[0]
    for k in range(1, n_off):
        offset = k // P_SIZE * LZ + k % P_SIZE
        coupling_lat = coupling_lat + jnp.roll(affine_lanes[k], offset, axis=-1)
    half_rows = P_SIZE * P_SIZE
    scale_lat = jnp.tanh(coupling_lat[:half_rows]).reshape(P_SIZE, P_SIZE, LY * LZ)
    shift_lat = coupling_lat[half_rows:].reshape(P_SIZE, P_SIZE, LY * LZ)
    log_det = jnp.sum(jnp.where(frozen, 0.0, scale_lat))
    new_field = jnp.where(frozen, u, u * jnp.exp(scale_lat) + shift_lat)

    ahead_time = shifted(new_field[0:1].astype(jnp.bfloat16), "tm", -1).astype(jnp.float32)
    ahead_slab = shifted(new_field[:, 0:1].astype(jnp.bfloat16), "space", -1).astype(jnp.float32)
    next_time_field = jnp.concatenate([new_field[1:], ahead_time], axis=0)
    next_slab_field = jnp.concatenate([new_field[:, 1:], ahead_slab], axis=1)
    next_y_field = jnp.roll(new_field, -LZ, axis=2)
    next_z_field = jnp.where(
        lane % LZ == LZ - 1, jnp.roll(new_field, LZ - 1, axis=2), jnp.roll(new_field, -1, axis=2)
    )
    neighbours = next_time_field + next_slab_field
    neighbours = neighbours + next_y_field
    neighbours = neighbours + next_z_field
    squared = new_field * new_field
    density = (
        -2.0 * hopping * new_field * neighbours
        + squared
        + quartic * (squared - 1.0) * (squared - 1.0)
    )
    time_link = new_field * next_time_field
    slab_link = new_field * next_slab_field
    local_log = -0.5 * jnp.sum(u * u) - log_det
    local_act = jnp.sum(density)
    members = lax.axis_size("space") * lax.axis_size("tm")
    partials = jnp.broadcast_to(jnp.stack([local_log, local_act])[None], (members, 2))
    sums = jnp.sum(lax.all_to_all(partials, ("space", "tm"), 0, 0, tiled=True), axis=0)
    sum_log, sum_act = sums[0], sums[1]
    site_count = u.size * lax.axis_size("space") * lax.axis_size("tm")
    totals = jnp.stack([sum_log / site_count - 0.5 * log_two_pi, sum_act / site_count]).astype(
        jnp.float32
    )
    return (new_field, density, time_link, slab_link, totals)


def solution(mesh):
    in_specs = (
        P("tm", "space", None),
        P("tm", "space", None),
        P(),
        P(),
        P(),
        P(),
        P(),
        P(),
        P(),
        P(),
    )
    out_specs = (
        P("tm", "space", None),
        P("tm", "space", None),
        P("tm", "space", None),
        P("tm", "space", None),
        P(),
    )
    return jax.shard_map(shards, mesh=mesh, in_specs=in_specs, out_specs=out_specs, check_vma=False)
```

```python
import math

import numpy as np
import jax
import jax.numpy as jnp
from jax import lax
from jax.sharding import PartitionSpec as P

P_SIZE = 4
D = 768
HEADS = 12
HS = 64
LY = 32
LZ = 64
BLK = 128


hopping = 0.2
quartic = 0.5
epsilon = 1e-05
log_two_pi = math.log(2.0 * math.pi)


def exchange(x, axis, bit):
    length = lax.axis_size(axis)
    return lax.ppermute(x, axis, [(i, i ^ bit) for i in range(length)])


def doubling_sum(x, axis):
    bit = 1
    while bit < lax.axis_size(axis):
        x = x + exchange(x, axis, bit)
        bit *= 2
    return x


def doubling_gather(x, axis):
    bits = []
    bit = 1
    while bit < lax.axis_size(axis):
        bits.append(bit)
        bit *= 2
    offsets = [0]
    for bit in reversed(bits[1:]):
        x = jnp.concatenate([x, exchange(x, axis, bit)], axis=0)
        offsets = offsets + [o ^ bit for o in offsets]
    received = exchange(x, axis, bits[0])
    offsets = offsets + [o ^ bits[0] for o in offsets]
    return x, received, offsets


def shifted(x, axis, by):
    length = lax.axis_size(axis)
    return lax.ppermute(x, axis, [(i, (i + by) % length) for i in range(length)])


def layer_norm(values, gain_vec):
    centre = values - jnp.mean(values, axis=-1, keepdims=True)
    spread = jnp.mean(centre * centre, axis=-1, keepdims=True)
    return centre * lax.rsqrt(spread + epsilon) * gain_vec


def site_parity(patch_side):
    positions = np.arange(patch_side**4, dtype=np.int32)
    return (
        positions // patch_side**3
        + positions // patch_side**2 % patch_side
        + positions // patch_side % patch_side
        + positions % patch_side
    ) % 2


def packed_rows(p_bit):
    th, x4, y4, z4 = np.meshgrid(np.arange(2), np.arange(4), np.arange(4), np.arange(4), indexing="ij")
    t4 = 2 * th + (p_bit + x4 + y4 + z4) % 2
    return (((t4 * 4 + x4) * 4 + y4) * 4 + z4).reshape(-1)


def embed_packed(tokens, bits, w_pair, b_embed):
    both = jnp.dot(tokens, w_pair, preferred_element_type=jnp.float32)
    half = both.shape[-1] // 2
    return jnp.where(bits[..., None] > 0.5, both[..., half:], both[..., :half]) + b_embed


def shards(
    lattice_field, parity, block_list, w_embed, b_embed, gain_in, w_qkv, gain_out, w_head, b_head
):
    n_y = LY // P_SIZE
    n_z = LZ // P_SIZE
    tokens_dev = n_y * n_z
    patch_len = P_SIZE**4
    u = lattice_field
    bits = parity.reshape(n_y, n_z)

    lane = lax.broadcasted_iota(jnp.int32, u.shape, 2)
    t_pos = lax.broadcasted_iota(jnp.int32, u.shape, 0)
    x_pos = lax.broadcasted_iota(jnp.int32, u.shape, 1)
    site_bit = (t_pos + x_pos + lane // LZ + lane % LZ) % 2
    bits_lat = jnp.repeat(jnp.repeat(bits, P_SIZE, axis=0), P_SIZE, axis=1).reshape(LY * LZ)
    frozen = site_bit == bits_lat[None, None, :]
    frozen_in = jnp.where(frozen, u, 0.0).astype(jnp.bfloat16)

    packed = frozen_in[0::2] + frozen_in[1::2]
    n_off = P_SIZE * P_SIZE
    tok_ids = lax.broadcasted_iota(jnp.int32, (tokens_dev, LY * LZ), 0)
    lane_ids = lax.broadcasted_iota(jnp.int32, (tokens_dev, LY * LZ), 1)
    tok_lane = tok_ids // n_z * (P_SIZE * LZ) + tok_ids % n_z * P_SIZE
    spread_tok = (lane_ids == tok_lane).astype(jnp.bfloat16)
    packed_rows_lat = packed.reshape(2 * P_SIZE, LY * LZ)
    shifted_rows = jnp.stack(
        [
            jnp.roll(packed_rows_lat, -(k // P_SIZE * LZ + k % P_SIZE), axis=-1)
            for k in range(n_off)
        ],
        axis=1,
    ).reshape(2 * P_SIZE * n_off, LY * LZ)
    tokens = jnp.einsum(
        "fl,tl->tf", shifted_rows, spread_tok, preferred_element_type=jnp.float32
    ).astype(jnp.bfloat16)
    bits_f = bits.reshape(1, tokens_dev).astype(jnp.bfloat16)
    send = jnp.concatenate([tokens, bits_f], axis=0)
    kept, received, offsets = doubling_gather(send[None], "tm")
    slot_of = np.argsort(np.asarray(offsets)).astype(np.int32)

    w_pair = jnp.concatenate(
        [w_embed[packed_rows(0)], w_embed[packed_rows(1)]], axis=1
    )
    bits_own = bits.reshape(tokens_dev).astype(jnp.float32)
    embedded = embed_packed(tokens, bits_own, w_pair, b_embed)
    normed = layer_norm(embedded, gain_in).astype(jnp.bfloat16)

    block_rows = lax.dynamic_index_in_dim(block_list, lax.axis_index("tm"), 0, keepdims=False)
    own = lax.axis_index("tm")
    slots = jnp.asarray(slot_of)[block_rows ^ own]
    n_half = kept.shape[0]
    half_ids = jnp.arange(n_half, dtype=jnp.int32)[None, :]
    pick_kept = (slots[:, None] == half_ids).astype(jnp.bfloat16)
    pick_received = (slots[:, None] == half_ids + n_half).astype(jnp.bfloat16)
    chosen = (
        jnp.einsum("ip,pab->iab", pick_kept, kept, preferred_element_type=jnp.float32)
        + jnp.einsum("ip,pab->iab", pick_received, received, preferred_element_type=jnp.float32)
    ).astype(jnp.bfloat16)
    n_sel = chosen.shape[0]
    sel_tokens = chosen[:, :tokens_dev, :].reshape(n_sel * tokens_dev, patch_len // 2)
    sel_bits = chosen[:, tokens_dev, :].reshape(n_sel * tokens_dev).astype(jnp.float32)
    sel_embedded = embed_packed(sel_tokens, sel_bits, w_pair, b_embed)
    sel_normed = layer_norm(sel_embedded, gain_in).astype(jnp.bfloat16)
    queries = jnp.dot(normed, w_qkv[:, :D], preferred_element_type=jnp.float32).astype(
        jnp.bfloat16
    )
    w_kv = w_qkv[:, D:].reshape(D, 2, HEADS, HS)
    kv = jnp.einsum(
        "tc,cnhd->nhtd", sel_normed, w_kv, preferred_element_type=jnp.float32
    ).astype(jnp.bfloat16)
    keys = kv[0]
    values = kv[1]

    scores = jnp.einsum(
        "qhd,hkd->hqk",
        queries.reshape(tokens_dev, HEADS, HS),
        keys,
        preferred_element_type=jnp.float32,
    ) * HS ** (-0.5)
    row_top = jnp.max(scores, axis=-1, keepdims=True)
    exp_scores = jnp.exp(scores - row_top)
    row_total = jnp.sum(exp_scores, axis=-1)
    product = jnp.einsum(
        "hqk,hkd->qhd",
        exp_scores.astype(jnp.bfloat16),
        values,
        preferred_element_type=jnp.float32,
    )
    mixed = (product / row_total.T[:, :, None]).reshape(tokens_dev, D)
    hidden = embedded + mixed
    normed_out = layer_norm(hidden, gain_out).astype(jnp.bfloat16)
    w_rows = w_head.reshape(D, 2 * P_SIZE * P_SIZE, n_off)
    affine_rows = jnp.einsum(
        "tc,crk->krt", normed_out, w_rows, preferred_element_type=jnp.float32
    ) + b_head.reshape(2 * P_SIZE * P_SIZE, n_off).T[:, :, None]
    high = lax.reduce_precision(affine_rows, exponent_bits=8, mantissa_bits=7)
    rest = affine_rows - high
    middle = lax.reduce_precision(rest, exponent_bits=8, mantissa_bits=7)
    low = rest - middle
    pieces = jnp.concatenate([high, middle, low], axis=-1).astype(jnp.bfloat16)
    spread_three = jnp.concatenate([spread_tok, spread_tok, spread_tok], axis=0)
    affine_lanes = jnp.einsum(
        "krt,tl->krl", pieces, spread_three, preferred_element_type=jnp.float32
    )
    coupling_lat = affine_lanes[0]
    for k in range(1, n_off):
        offset = k // P_SIZE * LZ + k % P_SIZE
        coupling_lat = coupling_lat + jnp.roll(affine_lanes[k], offset, axis=-1)
    half_rows = P_SIZE * P_SIZE
    scale_lat = jnp.tanh(coupling_lat[:half_rows]).reshape(P_SIZE, P_SIZE, LY * LZ)
    shift_lat = coupling_lat[half_rows:].reshape(P_SIZE, P_SIZE, LY * LZ)
    log_det = jnp.sum(jnp.where(frozen, 0.0, scale_lat))
    new_field = jnp.where(frozen, u, u * jnp.exp(scale_lat) + shift_lat)

    ahead_time = shifted(new_field[0:1].astype(jnp.bfloat16), "tm", -1).astype(jnp.float32)
    ahead_slab = shifted(new_field[:, 0:1].astype(jnp.bfloat16), "space", -1).astype(jnp.float32)
    next_time_field = jnp.concatenate([new_field[1:], ahead_time], axis=0)
    next_slab_field = jnp.concatenate([new_field[:, 1:], ahead_slab], axis=1)
    next_y_field = jnp.roll(new_field, -LZ, axis=2)
    next_z_field = jnp.where(
        lane % LZ == LZ - 1, jnp.roll(new_field, LZ - 1, axis=2), jnp.roll(new_field, -1, axis=2)
    )
    neighbours = next_time_field + next_slab_field
    neighbours = neighbours + next_y_field
    neighbours = neighbours + next_z_field
    squared = new_field * new_field
    density = (
        -2.0 * hopping * new_field * neighbours
        + squared
        + quartic * (squared - 1.0) * (squared - 1.0)
    )
    time_link = new_field * next_time_field
    slab_link = new_field * next_slab_field
    local_log = -0.5 * jnp.sum(u * u) - log_det
    local_act = jnp.sum(density)
    members = lax.axis_size("space") * lax.axis_size("tm")
    partials = jnp.broadcast_to(jnp.stack([local_log, local_act])[None], (members, 2))
    sums = jnp.sum(lax.all_to_all(partials, ("space", "tm"), 0, 0, tiled=True), axis=0)
    sum_log, sum_act = sums[0], sums[1]
    site_count = u.size * lax.axis_size("space") * lax.axis_size("tm")
    totals = jnp.stack([sum_log / site_count - 0.5 * log_two_pi, sum_act / site_count]).astype(
        jnp.float32
    )
    return (new_field, density, time_link, slab_link, totals)


def solution(mesh):
    in_specs = (
        P("tm", "space", None),
        P("tm", "space", None),
        P(),
        P(),
        P(),
        P(),
        P(),
        P(),
        P(),
        P(),
    )
    out_specs = (
        P("tm", "space", None),
        P("tm", "space", None),
        P("tm", "space", None),
        P("tm", "space", None),
        P(),
    )
    return jax.shard_map(shards, mesh=mesh, in_specs=in_specs, out_specs=out_specs, check_vma=False)
```

```python
import math

import numpy as np
import jax
import jax.numpy as jnp
from jax import lax
from jax.sharding import PartitionSpec as P

P_SIZE = 4
D = 768
HEADS = 12
HS = 64
LY = 32
LZ = 64
BLK = 128


hopping = 0.2
quartic = 0.5
epsilon = 1e-05
log_two_pi = math.log(2.0 * math.pi)


def exchange(x, axis, bit):
    length = lax.axis_size(axis)
    return lax.ppermute(x, axis, [(i, i ^ bit) for i in range(length)])


def doubling_sum(x, axis):
    bit = 1
    while bit < lax.axis_size(axis):
        x = x + exchange(x, axis, bit)
        bit *= 2
    return x


def doubling_gather(x, axis):
    bits = []
    bit = 1
    while bit < lax.axis_size(axis):
        bits.append(bit)
        bit *= 2
    offsets = [0]
    for bit in reversed(bits[1:]):
        x = jnp.concatenate([x, exchange(x, axis, bit)], axis=0)
        offsets = offsets + [o ^ bit for o in offsets]
    received = exchange(x, axis, bits[0])
    offsets = offsets + [o ^ bits[0] for o in offsets]
    return x, received, offsets


def shifted(x, axis, by):
    length = lax.axis_size(axis)
    return lax.ppermute(x, axis, [(i, (i + by) % length) for i in range(length)])


def layer_norm(values, gain_vec):
    centre = values - jnp.mean(values, axis=-1, keepdims=True)
    spread = jnp.mean(centre * centre, axis=-1, keepdims=True)
    return centre * lax.rsqrt(spread + epsilon) * gain_vec


def site_parity(patch_side):
    positions = np.arange(patch_side**4, dtype=np.int32)
    return (
        positions // patch_side**3
        + positions // patch_side**2 % patch_side
        + positions // patch_side % patch_side
        + positions % patch_side
    ) % 2


def packed_rows(p_bit):
    th, x4, y4, z4 = np.meshgrid(np.arange(2), np.arange(4), np.arange(4), np.arange(4), indexing="ij")
    t4 = 2 * th + (p_bit + x4 + y4 + z4) % 2
    return (((t4 * 4 + x4) * 4 + y4) * 4 + z4).reshape(-1)


def embed_packed(tokens, bits, w_pair, b_embed):
    both = jnp.dot(tokens, w_pair, preferred_element_type=jnp.float32)
    half = both.shape[-1] // 2
    return jnp.where(bits[..., None] > 0.5, both[..., half:], both[..., :half]) + b_embed


def shards(
    lattice_field, parity, block_list, w_embed, b_embed, gain_in, w_qkv, gain_out, w_head, b_head
):
    n_y = LY // P_SIZE
    n_z = LZ // P_SIZE
    tokens_dev = n_y * n_z
    patch_len = P_SIZE**4
    u = lattice_field
    bits = parity.reshape(n_y, n_z)

    lane = lax.broadcasted_iota(jnp.int32, u.shape, 2)
    t_pos = lax.broadcasted_iota(jnp.int32, u.shape, 0)
    x_pos = lax.broadcasted_iota(jnp.int32, u.shape, 1)
    site_bit = (t_pos + x_pos + lane // LZ + lane % LZ) % 2
    bits_lat = jnp.repeat(jnp.repeat(bits, P_SIZE, axis=0), P_SIZE, axis=1).reshape(LY * LZ)
    frozen = site_bit == bits_lat[None, None, :]
    frozen_in = jnp.where(frozen, u, 0.0).astype(jnp.bfloat16)

    packed = frozen_in[0::2] + frozen_in[1::2]
    n_off = P_SIZE * P_SIZE
    tok_ids = lax.broadcasted_iota(jnp.int32, (tokens_dev, LY * LZ), 0)
    lane_ids = lax.broadcasted_iota(jnp.int32, (tokens_dev, LY * LZ), 1)
    tok_lane = tok_ids // n_z * (P_SIZE * LZ) + tok_ids % n_z * P_SIZE
    spread_tok = (lane_ids == tok_lane).astype(jnp.bfloat16)
    packed_rows_lat = packed.reshape(2 * P_SIZE, LY * LZ)
    shifted_rows = jnp.stack(
        [
            jnp.roll(packed_rows_lat, -(k // P_SIZE * LZ + k % P_SIZE), axis=-1)
            for k in range(n_off)
        ],
        axis=1,
    ).reshape(2 * P_SIZE * n_off, LY * LZ)
    tokens = jnp.einsum(
        "fl,tl->tf", shifted_rows, spread_tok, preferred_element_type=jnp.float32
    ).astype(jnp.bfloat16)
    bits_f = bits.reshape(1, tokens_dev).astype(jnp.bfloat16)
    send = jnp.concatenate([tokens, bits_f], axis=0)
    kept, received, offsets = doubling_gather(send[None], "tm")
    slot_of = np.argsort(np.asarray(offsets)).astype(np.int32)

    w_pair = jnp.concatenate(
        [w_embed[packed_rows(0)], w_embed[packed_rows(1)]], axis=1
    )
    bits_own = bits.reshape(tokens_dev).astype(jnp.float32)
    embedded = embed_packed(tokens, bits_own, w_pair, b_embed)
    normed = layer_norm(embedded, gain_in).astype(jnp.bfloat16)

    block_rows = lax.dynamic_index_in_dim(block_list, lax.axis_index("tm"), 0, keepdims=False)
    own = lax.axis_index("tm")
    slots = jnp.asarray(slot_of)[block_rows ^ own]
    n_half = kept.shape[0]
    half_ids = jnp.arange(n_half, dtype=jnp.int32)[None, :]
    pick_kept = (slots[:, None] == half_ids).astype(jnp.bfloat16)
    pick_received = (slots[:, None] == half_ids + n_half).astype(jnp.bfloat16)
    chosen = (
        jnp.einsum("ip,pab->iab", pick_kept, kept, preferred_element_type=jnp.float32)
        + jnp.einsum("ip,pab->iab", pick_received, received, preferred_element_type=jnp.float32)
    ).astype(jnp.bfloat16)
    n_sel = chosen.shape[0]
    sel_tokens = chosen[:, :tokens_dev, :].reshape(n_sel * tokens_dev, patch_len // 2)
    sel_bits = chosen[:, tokens_dev, :].reshape(n_sel * tokens_dev).astype(jnp.float32)
    sel_embedded = embed_packed(sel_tokens, sel_bits, w_pair, b_embed)
    sel_normed = layer_norm(sel_embedded, gain_in).astype(jnp.bfloat16)
    queries = jnp.einsum(
        "tc,chd->htd", normed, w_qkv[:, :D].reshape(D, HEADS, HS),
        preferred_element_type=jnp.float32,
    ).astype(jnp.bfloat16)
    w_kv = w_qkv[:, D:].reshape(D, 2, HEADS, HS)
    kv = jnp.einsum(
        "tc,cnhd->nhtd", sel_normed, w_kv, preferred_element_type=jnp.float32
    ).astype(jnp.bfloat16)
    keys = kv[0]
    values = kv[1]

    scores = jnp.einsum(
        "hqd,hkd->hqk",
        queries,
        keys,
        preferred_element_type=jnp.float32,
    ) * HS ** (-0.5)
    row_top = jnp.max(scores, axis=-1, keepdims=True)
    exp_scores = jnp.exp(scores - row_top)
    row_total = jnp.sum(exp_scores, axis=-1)
    product = jnp.einsum(
        "hqk,hkd->qhd",
        exp_scores.astype(jnp.bfloat16),
        values,
        preferred_element_type=jnp.float32,
    )
    mixed = (product / row_total.T[:, :, None]).reshape(tokens_dev, D)
    hidden = embedded + mixed
    normed_out = layer_norm(hidden, gain_out).astype(jnp.bfloat16)
    w_rows = w_head.reshape(D, 2 * P_SIZE * P_SIZE, n_off)
    affine_rows = jnp.einsum(
        "tc,crk->krt", normed_out, w_rows, preferred_element_type=jnp.float32
    ) + b_head.reshape(2 * P_SIZE * P_SIZE, n_off).T[:, :, None]
    high = lax.reduce_precision(affine_rows, exponent_bits=8, mantissa_bits=7)
    rest = affine_rows - high
    middle = lax.reduce_precision(rest, exponent_bits=8, mantissa_bits=7)
    low = rest - middle
    pieces = jnp.concatenate([high, middle, low], axis=-1).astype(jnp.bfloat16)
    spread_three = jnp.concatenate([spread_tok, spread_tok, spread_tok], axis=0)
    affine_lanes = jnp.einsum(
        "krt,tl->krl", pieces, spread_three, preferred_element_type=jnp.float32
    )
    coupling_lat = affine_lanes[0]
    for k in range(1, n_off):
        offset = k // P_SIZE * LZ + k % P_SIZE
        coupling_lat = coupling_lat + jnp.roll(affine_lanes[k], offset, axis=-1)
    half_rows = P_SIZE * P_SIZE
    scale_lat = jnp.tanh(coupling_lat[:half_rows]).reshape(P_SIZE, P_SIZE, LY * LZ)
    shift_lat = coupling_lat[half_rows:].reshape(P_SIZE, P_SIZE, LY * LZ)
    log_det = jnp.sum(jnp.where(frozen, 0.0, scale_lat))
    new_field = jnp.where(frozen, u, u * jnp.exp(scale_lat) + shift_lat)

    ahead_time = shifted(new_field[0:1].astype(jnp.bfloat16), "tm", -1).astype(jnp.float32)
    ahead_slab = shifted(new_field[:, 0:1].astype(jnp.bfloat16), "space", -1).astype(jnp.float32)
    next_time_field = jnp.concatenate([new_field[1:], ahead_time], axis=0)
    next_slab_field = jnp.concatenate([new_field[:, 1:], ahead_slab], axis=1)
    next_y_field = jnp.roll(new_field, -LZ, axis=2)
    next_z_field = jnp.where(
        lane % LZ == LZ - 1, jnp.roll(new_field, LZ - 1, axis=2), jnp.roll(new_field, -1, axis=2)
    )
    neighbours = next_time_field + next_slab_field
    neighbours = neighbours + next_y_field
    neighbours = neighbours + next_z_field
    squared = new_field * new_field
    density = (
        -2.0 * hopping * new_field * neighbours
        + squared
        + quartic * (squared - 1.0) * (squared - 1.0)
    )
    time_link = new_field * next_time_field
    slab_link = new_field * next_slab_field
    local_log = -0.5 * jnp.sum(u * u) - log_det
    local_act = jnp.sum(density)
    members = lax.axis_size("space") * lax.axis_size("tm")
    partials = jnp.broadcast_to(jnp.stack([local_log, local_act])[None], (members, 2))
    sums = jnp.sum(lax.all_to_all(partials, ("space", "tm"), 0, 0, tiled=True), axis=0)
    sum_log, sum_act = sums[0], sums[1]
    site_count = u.size * lax.axis_size("space") * lax.axis_size("tm")
    totals = jnp.stack([sum_log / site_count - 0.5 * log_two_pi, sum_act / site_count]).astype(
        jnp.float32
    )
    return (new_field, density, time_link, slab_link, totals)


def solution(mesh):
    in_specs = (
        P("tm", "space", None),
        P("tm", "space", None),
        P(),
        P(),
        P(),
        P(),
        P(),
        P(),
        P(),
        P(),
    )
    out_specs = (
        P("tm", "space", None),
        P("tm", "space", None),
        P("tm", "space", None),
        P("tm", "space", None),
        P(),
    )
    return jax.shard_map(shards, mesh=mesh, in_specs=in_specs, out_specs=out_specs, check_vma=False)
```

```python
import math

import numpy as np
import jax
import jax.numpy as jnp
from jax import lax
from jax.sharding import PartitionSpec as P

P_SIZE = 4
D = 768
HEADS = 12
HS = 64
LY = 32
LZ = 64
BLK = 128


hopping = 0.2
quartic = 0.5
epsilon = 1e-05
log_two_pi = math.log(2.0 * math.pi)


def exchange(x, axis, bit):
    length = lax.axis_size(axis)
    return lax.ppermute(x, axis, [(i, i ^ bit) for i in range(length)])


def doubling_sum(x, axis):
    bit = 1
    while bit < lax.axis_size(axis):
        x = x + exchange(x, axis, bit)
        bit *= 2
    return x


def doubling_gather(x, axis):
    bits = []
    bit = 1
    while bit < lax.axis_size(axis):
        bits.append(bit)
        bit *= 2
    offsets = [0]
    for bit in reversed(bits[1:]):
        x = jnp.concatenate([x, exchange(x, axis, bit)], axis=0)
        offsets = offsets + [o ^ bit for o in offsets]
    received = exchange(x, axis, bits[0])
    offsets = offsets + [o ^ bits[0] for o in offsets]
    return x, received, offsets


def shifted(x, axis, by):
    length = lax.axis_size(axis)
    return lax.ppermute(x, axis, [(i, (i + by) % length) for i in range(length)])


def layer_norm(values, gain_vec):
    centre = values - jnp.mean(values, axis=-1, keepdims=True)
    spread = jnp.mean(centre * centre, axis=-1, keepdims=True)
    return centre * lax.rsqrt(spread + epsilon) * gain_vec


def site_parity(patch_side):
    positions = np.arange(patch_side**4, dtype=np.int32)
    return (
        positions // patch_side**3
        + positions // patch_side**2 % patch_side
        + positions // patch_side % patch_side
        + positions % patch_side
    ) % 2


def packed_rows(p_bit):
    th, x4, y4, z4 = np.meshgrid(np.arange(2), np.arange(4), np.arange(4), np.arange(4), indexing="ij")
    t4 = 2 * th + (p_bit + x4 + y4 + z4) % 2
    return (((t4 * 4 + x4) * 4 + y4) * 4 + z4).reshape(-1)


def embed_packed(tokens, bits, w_pair, b_embed):
    both = jnp.dot(tokens, w_pair, preferred_element_type=jnp.float32)
    half = both.shape[-1] // 2
    return jnp.where(bits[..., None] > 0.5, both[..., half:], both[..., :half]) + b_embed


def shards(
    lattice_field, parity, block_list, w_embed, b_embed, gain_in, w_qkv, gain_out, w_head, b_head
):
    n_y = LY // P_SIZE
    n_z = LZ // P_SIZE
    tokens_dev = n_y * n_z
    patch_len = P_SIZE**4
    u = lattice_field
    bits = parity.reshape(n_y, n_z)

    lane = lax.broadcasted_iota(jnp.int32, u.shape, 2)
    t_pos = lax.broadcasted_iota(jnp.int32, u.shape, 0)
    x_pos = lax.broadcasted_iota(jnp.int32, u.shape, 1)
    site_bit = (t_pos + x_pos + lane // LZ + lane % LZ) % 2
    bits_lat = jnp.repeat(jnp.repeat(bits, P_SIZE, axis=0), P_SIZE, axis=1).reshape(LY * LZ)
    frozen = site_bit == bits_lat[None, None, :]
    frozen_in = jnp.where(frozen, u, 0.0).astype(jnp.bfloat16)

    packed = frozen_in[0::2] + frozen_in[1::2]
    n_off = P_SIZE * P_SIZE
    tok_ids = lax.broadcasted_iota(jnp.int32, (tokens_dev, LY * LZ), 0)
    lane_ids = lax.broadcasted_iota(jnp.int32, (tokens_dev, LY * LZ), 1)
    tok_lane = tok_ids // n_z * (P_SIZE * LZ) + tok_ids % n_z * P_SIZE
    spread_tok = (lane_ids == tok_lane).astype(jnp.bfloat16)
    packed_rows_lat = packed.reshape(2 * P_SIZE, LY * LZ)
    shifted_rows = jnp.stack(
        [
            jnp.roll(packed_rows_lat, -(k // P_SIZE * LZ + k % P_SIZE), axis=-1)
            for k in range(n_off)
        ],
        axis=1,
    ).reshape(2 * P_SIZE * n_off, LY * LZ)
    tokens = jnp.einsum(
        "fl,tl->tf", shifted_rows, spread_tok, preferred_element_type=jnp.float32
    ).astype(jnp.bfloat16)
    bits_f = bits.reshape(1, tokens_dev).astype(jnp.bfloat16)
    send = jnp.concatenate([tokens, bits_f], axis=0)
    kept, received, offsets = doubling_gather(send[None], "tm")
    slot_of = np.argsort(np.asarray(offsets)).astype(np.int32)

    w_pair = jnp.concatenate(
        [w_embed[packed_rows(0)], w_embed[packed_rows(1)]], axis=1
    )
    bits_own = bits.reshape(tokens_dev).astype(jnp.float32)
    embedded = embed_packed(tokens, bits_own, w_pair, b_embed)
    normed = layer_norm(embedded, gain_in).astype(jnp.bfloat16)

    block_rows = lax.dynamic_index_in_dim(block_list, lax.axis_index("tm"), 0, keepdims=False)
    own = lax.axis_index("tm")
    slots = jnp.asarray(slot_of)[block_rows ^ own]
    n_half = kept.shape[0]
    half_ids = jnp.arange(n_half, dtype=jnp.int32)[None, :]
    pick_kept = (slots[:, None] == half_ids).astype(jnp.bfloat16)
    pick_received = (slots[:, None] == half_ids + n_half).astype(jnp.bfloat16)
    chosen = (
        jnp.einsum("ip,pab->iab", pick_kept, kept, preferred_element_type=jnp.float32)
        + jnp.einsum("ip,pab->iab", pick_received, received, preferred_element_type=jnp.float32)
    ).astype(jnp.bfloat16)
    n_sel = chosen.shape[0]
    sel_tokens = chosen[:, :tokens_dev, :].reshape(n_sel * tokens_dev, patch_len // 2)
    sel_bits = chosen[:, tokens_dev, :].reshape(n_sel * tokens_dev).astype(jnp.float32)
    sel_embedded = embed_packed(sel_tokens, sel_bits, w_pair, b_embed)
    sel_normed = layer_norm(sel_embedded, gain_in).astype(jnp.bfloat16)
    queries = jnp.einsum(
        "tc,chd->htd", normed, w_qkv[:, :D].reshape(D, HEADS, HS),
        preferred_element_type=jnp.float32,
    ).astype(jnp.bfloat16)
    w_kv = w_qkv[:, D:].reshape(D, 2, HEADS, HS)
    kv = jnp.einsum(
        "tc,cnhd->nhtd", sel_normed, w_kv, preferred_element_type=jnp.float32
    ).astype(jnp.bfloat16)
    keys = kv[0]
    values = kv[1]

    scores = jnp.einsum(
        "hqd,hkd->hqk",
        queries,
        keys,
        preferred_element_type=jnp.float32,
    ) * HS ** (-0.5)
    row_top = jnp.max(scores, axis=-1, keepdims=True)
    exp_scores = jnp.exp(scores - row_top)
    row_total = jnp.sum(exp_scores, axis=-1)
    product = jnp.einsum(
        "hqk,hkd->qhd",
        exp_scores.astype(jnp.bfloat16),
        values,
        preferred_element_type=jnp.float32,
    )
    mixed = (product / row_total.T[:, :, None]).reshape(tokens_dev, D)
    hidden = embedded + mixed
    normed_out = layer_norm(hidden, gain_out).astype(jnp.bfloat16)
    w_rows = w_head.reshape(D, 2 * P_SIZE * P_SIZE, n_off)
    affine_rows = jnp.einsum(
        "tc,crk->krt", normed_out, w_rows, preferred_element_type=jnp.float32
    ) + b_head.reshape(2 * P_SIZE * P_SIZE, n_off).T[:, :, None]
    high = lax.reduce_precision(affine_rows, exponent_bits=8, mantissa_bits=7)
    rest = affine_rows - high
    middle = lax.reduce_precision(rest, exponent_bits=8, mantissa_bits=7)
    low = rest - middle
    pieces = jnp.concatenate([high, middle, low], axis=-1).astype(jnp.bfloat16)
    spread_three = jnp.concatenate([spread_tok, spread_tok, spread_tok], axis=0)
    affine_lanes = jnp.einsum(
        "krt,tl->krl", pieces, spread_three, preferred_element_type=jnp.float32
    )
    coupling_lat = affine_lanes[0]
    for k in range(1, n_off):
        offset = k // P_SIZE * LZ + k % P_SIZE
        coupling_lat = coupling_lat + jnp.roll(affine_lanes[k], offset, axis=-1)
    half_rows = P_SIZE * P_SIZE
    scale_lat = jnp.tanh(coupling_lat[:half_rows]).reshape(P_SIZE, P_SIZE, LY * LZ)
    shift_lat = coupling_lat[half_rows:].reshape(P_SIZE, P_SIZE, LY * LZ)
    log_det = jnp.sum(jnp.where(frozen, 0.0, scale_lat))
    new_field = jnp.where(frozen, u, u * jnp.exp(scale_lat) + shift_lat)

    ahead_time = shifted(new_field[0:1].astype(jnp.bfloat16), "tm", -1)
    slab_plane, ahead_time = lax.optimization_barrier(
        (new_field[:, 0:1].astype(jnp.bfloat16), ahead_time)
    )
    ahead_time = ahead_time.astype(jnp.float32)
    ahead_slab = shifted(slab_plane, "space", -1).astype(jnp.float32)
    next_time_field = jnp.concatenate([new_field[1:], ahead_time], axis=0)
    next_slab_field = jnp.concatenate([new_field[:, 1:], ahead_slab], axis=1)
    next_y_field = jnp.roll(new_field, -LZ, axis=2)
    next_z_field = jnp.where(
        lane % LZ == LZ - 1, jnp.roll(new_field, LZ - 1, axis=2), jnp.roll(new_field, -1, axis=2)
    )
    neighbours = next_time_field + next_slab_field
    neighbours = neighbours + next_y_field
    neighbours = neighbours + next_z_field
    squared = new_field * new_field
    density = (
        -2.0 * hopping * new_field * neighbours
        + squared
        + quartic * (squared - 1.0) * (squared - 1.0)
    )
    time_link = new_field * next_time_field
    slab_link = new_field * next_slab_field
    local_log = -0.5 * jnp.sum(u * u) - log_det
    local_act = jnp.sum(density)
    members = lax.axis_size("space") * lax.axis_size("tm")
    partials = jnp.broadcast_to(jnp.stack([local_log, local_act])[None], (members, 2))
    sums = jnp.sum(lax.all_to_all(partials, ("space", "tm"), 0, 0, tiled=True), axis=0)
    sum_log, sum_act = sums[0], sums[1]
    site_count = u.size * lax.axis_size("space") * lax.axis_size("tm")
    totals = jnp.stack([sum_log / site_count - 0.5 * log_two_pi, sum_act / site_count]).astype(
        jnp.float32
    )
    return (new_field, density, time_link, slab_link, totals)


def solution(mesh):
    in_specs = (
        P("tm", "space", None),
        P("tm", "space", None),
        P(),
        P(),
        P(),
        P(),
        P(),
        P(),
        P(),
        P(),
    )
    out_specs = (
        P("tm", "space", None),
        P("tm", "space", None),
        P("tm", "space", None),
        P("tm", "space", None),
        P(),
    )
    return jax.shard_map(shards, mesh=mesh, in_specs=in_specs, out_specs=out_specs, check_vma=False)
```

```python
import math

import numpy as np
import jax
import jax.numpy as jnp
from jax import lax
from jax.sharding import PartitionSpec as P

P_SIZE = 4
D = 768
HEADS = 12
HS = 64
LY = 32
LZ = 64
BLK = 128


hopping = 0.2
quartic = 0.5
epsilon = 1e-05
log_two_pi = math.log(2.0 * math.pi)


def exchange(x, axis, bit):
    length = lax.axis_size(axis)
    return lax.ppermute(x, axis, [(i, i ^ bit) for i in range(length)])


def doubling_sum(x, axis):
    bit = 1
    while bit < lax.axis_size(axis):
        x = x + exchange(x, axis, bit)
        bit *= 2
    return x


def doubling_gather(x, axis):
    bits = []
    bit = 1
    while bit < lax.axis_size(axis):
        bits.append(bit)
        bit *= 2
    offsets = [0]
    for bit in reversed(bits[1:]):
        x = jnp.concatenate([x, exchange(x, axis, bit)], axis=0)
        offsets = offsets + [o ^ bit for o in offsets]
    received = exchange(x, axis, bits[0])
    offsets = offsets + [o ^ bits[0] for o in offsets]
    return x, received, offsets


def shifted(x, axis, by):
    length = lax.axis_size(axis)
    return lax.ppermute(x, axis, [(i, (i + by) % length) for i in range(length)])


def layer_norm(values, gain_vec):
    centre = values - jnp.mean(values, axis=-1, keepdims=True)
    spread = jnp.mean(centre * centre, axis=-1, keepdims=True)
    return centre * lax.rsqrt(spread + epsilon) * gain_vec


def layer_norm_heads(values, gain_vec):
    centre = values - jnp.mean(values, axis=(0, 2), keepdims=True)
    spread = jnp.mean(centre * centre, axis=(0, 2), keepdims=True)
    return centre * lax.rsqrt(spread + epsilon) * gain_vec.reshape(HEADS, 1, HS)


def site_parity(patch_side):
    positions = np.arange(patch_side**4, dtype=np.int32)
    return (
        positions // patch_side**3
        + positions // patch_side**2 % patch_side
        + positions // patch_side % patch_side
        + positions % patch_side
    ) % 2


def packed_rows(p_bit):
    th, x4, y4, z4 = np.meshgrid(np.arange(2), np.arange(4), np.arange(4), np.arange(4), indexing="ij")
    t4 = 2 * th + (p_bit + x4 + y4 + z4) % 2
    return (((t4 * 4 + x4) * 4 + y4) * 4 + z4).reshape(-1)


def embed_packed(tokens, bits, w_pair, b_embed):
    both = jnp.dot(tokens, w_pair, preferred_element_type=jnp.float32)
    half = both.shape[-1] // 2
    return jnp.where(bits[..., None] > 0.5, both[..., half:], both[..., :half]) + b_embed


def shards(
    lattice_field, parity, block_list, w_embed, b_embed, gain_in, w_qkv, gain_out, w_head, b_head
):
    n_y = LY // P_SIZE
    n_z = LZ // P_SIZE
    tokens_dev = n_y * n_z
    patch_len = P_SIZE**4
    u = lattice_field
    bits = parity.reshape(n_y, n_z)

    lane = lax.broadcasted_iota(jnp.int32, u.shape, 2)
    t_pos = lax.broadcasted_iota(jnp.int32, u.shape, 0)
    x_pos = lax.broadcasted_iota(jnp.int32, u.shape, 1)
    site_bit = (t_pos + x_pos + lane // LZ + lane % LZ) % 2
    bits_lat = jnp.repeat(jnp.repeat(bits, P_SIZE, axis=0), P_SIZE, axis=1).reshape(LY * LZ)
    frozen = site_bit == bits_lat[None, None, :]
    frozen_in = jnp.where(frozen, u, 0.0).astype(jnp.bfloat16)

    packed = frozen_in[0::2] + frozen_in[1::2]
    n_off = P_SIZE * P_SIZE
    tok_ids = lax.broadcasted_iota(jnp.int32, (tokens_dev, LY * LZ), 0)
    lane_ids = lax.broadcasted_iota(jnp.int32, (tokens_dev, LY * LZ), 1)
    tok_lane = tok_ids // n_z * (P_SIZE * LZ) + tok_ids % n_z * P_SIZE
    spread_tok = (lane_ids == tok_lane).astype(jnp.bfloat16)
    packed_rows_lat = packed.reshape(2 * P_SIZE, LY * LZ)
    shifted_rows = jnp.stack(
        [
            jnp.roll(packed_rows_lat, -(k // P_SIZE * LZ + k % P_SIZE), axis=-1)
            for k in range(n_off)
        ],
        axis=1,
    ).reshape(2 * P_SIZE * n_off, LY * LZ)
    tokens = jnp.einsum(
        "fl,tl->tf", shifted_rows, spread_tok, preferred_element_type=jnp.float32
    ).astype(jnp.bfloat16)
    bits_f = bits.reshape(1, tokens_dev).astype(jnp.bfloat16)
    send = jnp.concatenate([tokens, bits_f], axis=0)
    kept, received, offsets = doubling_gather(send[None], "tm")
    slot_of = np.argsort(np.asarray(offsets)).astype(np.int32)

    w_pair = jnp.concatenate(
        [w_embed[packed_rows(0)], w_embed[packed_rows(1)]], axis=1
    )
    bits_own = bits.reshape(tokens_dev).astype(jnp.float32)
    both_h = jnp.einsum(
        "tf,fshd->shtd", tokens, w_pair.reshape(patch_len // 2, 2, HEADS, HS),
        preferred_element_type=jnp.float32,
    )
    embedded_h = jnp.where(bits_own[None, :, None] > 0.5, both_h[1], both_h[0]) + b_embed.reshape(
        HEADS, 1, HS
    )
    normed_h = layer_norm_heads(embedded_h, gain_in).astype(jnp.bfloat16)

    block_rows = lax.dynamic_index_in_dim(block_list, lax.axis_index("tm"), 0, keepdims=False)
    own = lax.axis_index("tm")
    slots = jnp.asarray(slot_of)[block_rows ^ own]
    n_half = kept.shape[0]
    half_ids = jnp.arange(n_half, dtype=jnp.int32)[None, :]
    pick_kept = (slots[:, None] == half_ids).astype(jnp.bfloat16)
    pick_received = (slots[:, None] == half_ids + n_half).astype(jnp.bfloat16)
    chosen = (
        jnp.einsum("ip,pab->iab", pick_kept, kept, preferred_element_type=jnp.float32)
        + jnp.einsum("ip,pab->iab", pick_received, received, preferred_element_type=jnp.float32)
    ).astype(jnp.bfloat16)
    n_sel = chosen.shape[0]
    sel_tokens = chosen[:, :tokens_dev, :].reshape(n_sel * tokens_dev, patch_len // 2)
    sel_bits = chosen[:, tokens_dev, :].reshape(n_sel * tokens_dev).astype(jnp.float32)
    sel_embedded = embed_packed(sel_tokens, sel_bits, w_pair, b_embed)
    sel_normed = layer_norm(sel_embedded, gain_in).astype(jnp.bfloat16)
    queries = jnp.einsum(
        "gte,gehd->htd", normed_h, w_qkv[:, :D].reshape(HEADS, HS, HEADS, HS),
        preferred_element_type=jnp.float32,
    ).astype(jnp.bfloat16)
    w_kv = w_qkv[:, D:].reshape(D, 2, HEADS, HS)
    kv = jnp.einsum(
        "tc,cnhd->nhtd", sel_normed, w_kv, preferred_element_type=jnp.float32
    ).astype(jnp.bfloat16)
    keys = kv[0]
    values = kv[1]

    scores = jnp.einsum(
        "hqd,hkd->hqk",
        queries,
        keys,
        preferred_element_type=jnp.float32,
    ) * HS ** (-0.5)
    row_top = jnp.max(scores, axis=-1, keepdims=True)
    exp_scores = jnp.exp(scores - row_top)
    row_total = jnp.sum(exp_scores, axis=-1)
    product = jnp.einsum(
        "hqk,hkd->hqd",
        exp_scores.astype(jnp.bfloat16),
        values,
        preferred_element_type=jnp.float32,
    )
    hidden_h = embedded_h + product / row_total[:, :, None]
    normed_out_h = layer_norm_heads(hidden_h, gain_out).astype(jnp.bfloat16)
    w_rows = w_head.reshape(HEADS, HS, 2 * P_SIZE * P_SIZE, n_off)
    affine_rows = jnp.einsum(
        "htd,hdrk->krt", normed_out_h, w_rows, preferred_element_type=jnp.float32
    ) + b_head.reshape(2 * P_SIZE * P_SIZE, n_off).T[:, :, None]
    high = lax.reduce_precision(affine_rows, exponent_bits=8, mantissa_bits=7)
    rest = affine_rows - high
    middle = lax.reduce_precision(rest, exponent_bits=8, mantissa_bits=7)
    low = rest - middle
    pieces = jnp.concatenate([high, middle, low], axis=-1).astype(jnp.bfloat16)
    spread_three = jnp.concatenate([spread_tok, spread_tok, spread_tok], axis=0)
    affine_lanes = jnp.einsum(
        "krt,tl->krl", pieces, spread_three, preferred_element_type=jnp.float32
    )
    coupling_lat = affine_lanes[0]
    for k in range(1, n_off):
        offset = k // P_SIZE * LZ + k % P_SIZE
        coupling_lat = coupling_lat + jnp.roll(affine_lanes[k], offset, axis=-1)
    half_rows = P_SIZE * P_SIZE
    scale_lat = jnp.tanh(coupling_lat[:half_rows]).reshape(P_SIZE, P_SIZE, LY * LZ)
    shift_lat = coupling_lat[half_rows:].reshape(P_SIZE, P_SIZE, LY * LZ)
    log_det = jnp.sum(jnp.where(frozen, 0.0, scale_lat))
    new_field = jnp.where(frozen, u, u * jnp.exp(scale_lat) + shift_lat)

    ahead_time = shifted(new_field[0:1].astype(jnp.bfloat16), "tm", -1).astype(jnp.float32)
    ahead_slab = shifted(new_field[:, 0:1].astype(jnp.bfloat16), "space", -1).astype(jnp.float32)
    next_time_field = jnp.concatenate([new_field[1:], ahead_time], axis=0)
    next_slab_field = jnp.concatenate([new_field[:, 1:], ahead_slab], axis=1)
    next_y_field = jnp.roll(new_field, -LZ, axis=2)
    next_z_field = jnp.where(
        lane % LZ == LZ - 1, jnp.roll(new_field, LZ - 1, axis=2), jnp.roll(new_field, -1, axis=2)
    )
    neighbours = next_time_field + next_slab_field
    neighbours = neighbours + next_y_field
    neighbours = neighbours + next_z_field
    squared = new_field * new_field
    density = (
        -2.0 * hopping * new_field * neighbours
        + squared
        + quartic * (squared - 1.0) * (squared - 1.0)
    )
    time_link = new_field * next_time_field
    slab_link = new_field * next_slab_field
    local_log = -0.5 * jnp.sum(u * u) - log_det
    local_act = jnp.sum(density)
    members = lax.axis_size("space") * lax.axis_size("tm")
    partials = jnp.broadcast_to(jnp.stack([local_log, local_act])[None], (members, 2))
    sums = jnp.sum(lax.all_to_all(partials, ("space", "tm"), 0, 0, tiled=True), axis=0)
    sum_log, sum_act = sums[0], sums[1]
    site_count = u.size * lax.axis_size("space") * lax.axis_size("tm")
    totals = jnp.stack([sum_log / site_count - 0.5 * log_two_pi, sum_act / site_count]).astype(
        jnp.float32
    )
    return (new_field, density, time_link, slab_link, totals)


def solution(mesh):
    in_specs = (
        P("tm", "space", None),
        P("tm", "space", None),
        P(),
        P(),
        P(),
        P(),
        P(),
        P(),
        P(),
        P(),
    )
    out_specs = (
        P("tm", "space", None),
        P("tm", "space", None),
        P("tm", "space", None),
        P("tm", "space", None),
        P(),
    )
    return jax.shard_map(shards, mesh=mesh, in_specs=in_specs, out_specs=out_specs, check_vma=False)
```

```python
import math

import numpy as np
import jax
import jax.numpy as jnp
from jax import lax
from jax.sharding import PartitionSpec as P

P_SIZE = 4
D = 768
HEADS = 12
HS = 64
LY = 32
LZ = 64
BLK = 128


hopping = 0.2
quartic = 0.5
epsilon = 1e-05
log_two_pi = math.log(2.0 * math.pi)


def exchange(x, axis, bit):
    length = lax.axis_size(axis)
    return lax.ppermute(x, axis, [(i, i ^ bit) for i in range(length)])


def doubling_sum(x, axis):
    bit = 1
    while bit < lax.axis_size(axis):
        x = x + exchange(x, axis, bit)
        bit *= 2
    return x


def doubling_gather(x, axis):
    bits = []
    bit = 1
    while bit < lax.axis_size(axis):
        bits.append(bit)
        bit *= 2
    offsets = [0]
    for bit in reversed(bits[1:]):
        x = jnp.concatenate([x, exchange(x, axis, bit)], axis=0)
        offsets = offsets + [o ^ bit for o in offsets]
    received = exchange(x, axis, bits[0])
    offsets = offsets + [o ^ bits[0] for o in offsets]
    return x, received, offsets


def shifted(x, axis, by):
    length = lax.axis_size(axis)
    return lax.ppermute(x, axis, [(i, (i + by) % length) for i in range(length)])


def layer_norm(values, gain_vec):
    centre = values - jnp.mean(values, axis=-1, keepdims=True)
    spread = jnp.mean(centre * centre, axis=-1, keepdims=True)
    return centre * lax.rsqrt(spread + epsilon) * gain_vec


def site_parity(patch_side):
    positions = np.arange(patch_side**4, dtype=np.int32)
    return (
        positions // patch_side**3
        + positions // patch_side**2 % patch_side
        + positions // patch_side % patch_side
        + positions % patch_side
    ) % 2


def packed_rows(p_bit):
    th, x4, y4, z4 = np.meshgrid(np.arange(2), np.arange(4), np.arange(4), np.arange(4), indexing="ij")
    t4 = 2 * th + (p_bit + x4 + y4 + z4) % 2
    return (((t4 * 4 + x4) * 4 + y4) * 4 + z4).reshape(-1)


def embed_packed(tokens, bits, w_pair, b_embed):
    both = jnp.dot(tokens, w_pair, preferred_element_type=jnp.float32)
    half = both.shape[-1] // 2
    return jnp.where(bits[..., None] > 0.5, both[..., half:], both[..., :half]) + b_embed


def shards(
    lattice_field, parity, block_list, w_embed, b_embed, gain_in, w_qkv, gain_out, w_head, b_head
):
    n_y = LY // P_SIZE
    n_z = LZ // P_SIZE
    tokens_dev = n_y * n_z
    patch_len = P_SIZE**4
    u = lattice_field
    bits = parity.reshape(n_y, n_z)

    lane = lax.broadcasted_iota(jnp.int32, u.shape, 2)
    t_pos = lax.broadcasted_iota(jnp.int32, u.shape, 0)
    x_pos = lax.broadcasted_iota(jnp.int32, u.shape, 1)
    site_bit = (t_pos + x_pos + lane // LZ + lane % LZ) % 2
    bits_lat = jnp.repeat(jnp.repeat(bits, P_SIZE, axis=0), P_SIZE, axis=1).reshape(LY * LZ)
    frozen = site_bit == bits_lat[None, None, :]
    frozen_in = jnp.where(frozen, u, 0.0).astype(jnp.bfloat16)

    packed = frozen_in[0::2] + frozen_in[1::2]
    n_off = P_SIZE * P_SIZE
    tok_ids = lax.broadcasted_iota(jnp.int32, (tokens_dev, LY * LZ), 0)
    lane_ids = lax.broadcasted_iota(jnp.int32, (tokens_dev, LY * LZ), 1)
    tok_lane = tok_ids // n_z * (P_SIZE * LZ) + tok_ids % n_z * P_SIZE
    spread_tok = (lane_ids == tok_lane).astype(jnp.bfloat16)
    packed_rows_lat = packed.reshape(2 * P_SIZE, LY * LZ)
    shifted_rows = jnp.stack(
        [
            jnp.roll(packed_rows_lat, -(k // P_SIZE * LZ + k % P_SIZE), axis=-1)
            for k in range(n_off)
        ],
        axis=1,
    ).reshape(2 * P_SIZE * n_off, LY * LZ)
    tokens = jnp.einsum(
        "fl,tl->tf", shifted_rows, spread_tok, preferred_element_type=jnp.float32
    ).astype(jnp.bfloat16)
    bits_f = bits.reshape(1, tokens_dev).astype(jnp.bfloat16)
    send = jnp.concatenate([tokens, bits_f], axis=0)
    kept, received, offsets = doubling_gather(send[None], "tm")
    slot_of = np.argsort(np.asarray(offsets)).astype(np.int32)

    w_pair = jnp.concatenate(
        [w_embed[packed_rows(0)], w_embed[packed_rows(1)]], axis=1
    )
    bits_own = bits.reshape(tokens_dev).astype(jnp.float32)
    embedded = embed_packed(tokens, bits_own, w_pair, b_embed)
    normed = layer_norm(embedded, gain_in).astype(jnp.bfloat16)

    block_rows = lax.dynamic_index_in_dim(block_list, lax.axis_index("tm"), 0, keepdims=False)
    own = lax.axis_index("tm")
    slots = jnp.asarray(slot_of)[block_rows ^ own]
    n_half = kept.shape[0]
    half_ids = jnp.arange(n_half, dtype=jnp.int32)[None, :]
    pick_kept = (slots[:, None] == half_ids).astype(jnp.bfloat16)
    pick_received = (slots[:, None] == half_ids + n_half).astype(jnp.bfloat16)
    chosen = (
        jnp.einsum("ip,pab->iab", pick_kept, kept, preferred_element_type=jnp.float32)
        + jnp.einsum("ip,pab->iab", pick_received, received, preferred_element_type=jnp.float32)
    ).astype(jnp.bfloat16)
    n_sel = chosen.shape[0]
    sel_tokens = chosen[:, :tokens_dev, :].reshape(n_sel * tokens_dev, patch_len // 2)
    sel_bits = chosen[:, tokens_dev, :].reshape(n_sel * tokens_dev).astype(jnp.float32)
    sel_embedded = embed_packed(sel_tokens, sel_bits, w_pair, b_embed)
    sel_normed = layer_norm(sel_embedded, gain_in).astype(jnp.bfloat16)
    queries = jnp.einsum(
        "tc,chd->htd", normed, w_qkv[:, :D].reshape(D, HEADS, HS),
        preferred_element_type=jnp.float32,
    ).astype(jnp.bfloat16)
    w_kv = w_qkv[:, D:].reshape(D, 2, HEADS, HS)
    kv = jnp.einsum(
        "tc,cnhd->nhtd", sel_normed, w_kv, preferred_element_type=jnp.float32
    ).astype(jnp.bfloat16)
    keys = kv[0]
    values = kv[1]

    scores = jnp.einsum(
        "hqd,hkd->hqk",
        queries,
        keys,
        preferred_element_type=jnp.float32,
    ) * HS ** (-0.5)
    row_top = jnp.max(scores, axis=-1, keepdims=True)
    exp_scores = jnp.exp(scores - row_top)
    row_total = jnp.sum(exp_scores, axis=-1)
    product = jnp.einsum(
        "hqk,hkd->qhd",
        exp_scores.astype(jnp.bfloat16),
        values,
        preferred_element_type=jnp.float32,
    )
    mixed = (product / row_total.T[:, :, None]).reshape(tokens_dev, D)
    hidden = embedded + mixed
    normed_out = layer_norm(hidden, gain_out).astype(jnp.bfloat16)
    w_rows = w_head.reshape(D, 2 * P_SIZE * P_SIZE, n_off)
    affine_rows = jnp.einsum(
        "tc,crk->krt", normed_out, w_rows, preferred_element_type=jnp.float32
    ) + b_head.reshape(2 * P_SIZE * P_SIZE, n_off).T[:, :, None]
    high = lax.reduce_precision(affine_rows, exponent_bits=8, mantissa_bits=7)
    rest = affine_rows - high
    middle = lax.reduce_precision(rest, exponent_bits=8, mantissa_bits=7)
    low = rest - middle
    pieces = jnp.concatenate([high, middle, low], axis=-1).astype(jnp.bfloat16)
    spread_three = jnp.concatenate([spread_tok, spread_tok, spread_tok], axis=0)
    affine_lanes = jnp.einsum(
        "krt,tl->krl", pieces, spread_three, preferred_element_type=jnp.float32
    )
    coupling_lat = affine_lanes[0]
    for k in range(1, n_off):
        offset = k // P_SIZE * LZ + k % P_SIZE
        coupling_lat = coupling_lat + jnp.roll(affine_lanes[k], offset, axis=-1)
    half_rows = P_SIZE * P_SIZE
    scale_lat = jnp.tanh(coupling_lat[:half_rows]).reshape(P_SIZE, P_SIZE, LY * LZ)
    shift_lat = coupling_lat[half_rows:].reshape(P_SIZE, P_SIZE, LY * LZ)
    log_det = jnp.sum(jnp.where(frozen, 0.0, scale_lat))
    new_field = jnp.where(frozen, u, u * jnp.exp(scale_lat) + shift_lat)

    ahead_time = shifted(new_field[0:1].astype(jnp.bfloat16), "tm", -1).astype(jnp.float32)
    ahead_slab = shifted(new_field[:, 0:1].astype(jnp.bfloat16), "space", -1).astype(jnp.float32)
    next_time_field = jnp.concatenate([new_field[1:], ahead_time], axis=0)
    next_slab_field = jnp.concatenate([new_field[:, 1:], ahead_slab], axis=1)
    next_y_field = jnp.roll(new_field, -LZ, axis=2)
    next_z_field = jnp.where(
        lane % LZ == LZ - 1, jnp.roll(new_field, LZ - 1, axis=2), jnp.roll(new_field, -1, axis=2)
    )
    neighbours = next_time_field + next_slab_field
    neighbours = neighbours + next_y_field
    neighbours = neighbours + next_z_field
    squared = new_field * new_field
    density = (
        -2.0 * hopping * new_field * neighbours
        + squared
        + quartic * (squared - 1.0) * (squared - 1.0)
    )
    time_link = new_field * next_time_field
    slab_link = new_field * next_slab_field
    local_log = -0.5 * jnp.sum(u * u) - log_det
    on_site = squared + quartic * (squared - 1.0) * (squared - 1.0)
    inner = next_y_field + next_z_field
    inner_t = jnp.sum(new_field[:-1] * new_field[1:])
    inner_x = jnp.sum(new_field[:, :-1] * new_field[:, 1:])
    local_part = jnp.sum(on_site - 2.0 * hopping * new_field * inner) - 2.0 * hopping * (
        inner_t + inner_x
    )
    edge_part = jnp.sum(new_field[-1:] * ahead_time) + jnp.sum(new_field[:, -1:] * ahead_slab)
    local_act = local_part - 2.0 * hopping * edge_part
    members = lax.axis_size("space") * lax.axis_size("tm")
    partials = jnp.broadcast_to(jnp.stack([local_log, local_act])[None], (members, 2))
    sums = jnp.sum(lax.all_to_all(partials, ("space", "tm"), 0, 0, tiled=True), axis=0)
    sum_log, sum_act = sums[0], sums[1]
    site_count = u.size * lax.axis_size("space") * lax.axis_size("tm")
    totals = jnp.stack([sum_log / site_count - 0.5 * log_two_pi, sum_act / site_count]).astype(
        jnp.float32
    )
    return (new_field, density, time_link, slab_link, totals)


def solution(mesh):
    in_specs = (
        P("tm", "space", None),
        P("tm", "space", None),
        P(),
        P(),
        P(),
        P(),
        P(),
        P(),
        P(),
        P(),
    )
    out_specs = (
        P("tm", "space", None),
        P("tm", "space", None),
        P("tm", "space", None),
        P("tm", "space", None),
        P(),
    )
    return jax.shard_map(shards, mesh=mesh, in_specs=in_specs, out_specs=out_specs, check_vma=False)
```

```python
import math

import numpy as np
import jax
import jax.numpy as jnp
from jax import lax
from jax.sharding import PartitionSpec as P

P_SIZE = 4
D = 768
HEADS = 12
HS = 64
LY = 32
LZ = 64
BLK = 128


hopping = 0.2
quartic = 0.5
epsilon = 1e-05
log_two_pi = math.log(2.0 * math.pi)


def exchange(x, axis, bit):
    length = lax.axis_size(axis)
    return lax.ppermute(x, axis, [(i, i ^ bit) for i in range(length)])


def doubling_sum(x, axis):
    bit = 1
    while bit < lax.axis_size(axis):
        x = x + exchange(x, axis, bit)
        bit *= 2
    return x


def doubling_gather(x, axis):
    bits = []
    bit = 1
    while bit < lax.axis_size(axis):
        bits.append(bit)
        bit *= 2
    offsets = [0]
    for bit in bits[:-1]:
        x = jnp.concatenate([x, exchange(x, axis, bit)], axis=0)
        offsets = offsets + [o ^ bit for o in offsets]
    received = exchange(x, axis, bits[-1])
    offsets = offsets + [o ^ bits[-1] for o in offsets]
    return x, received, offsets


def shifted(x, axis, by):
    length = lax.axis_size(axis)
    return lax.ppermute(x, axis, [(i, (i + by) % length) for i in range(length)])


def layer_norm(values, gain_vec):
    centre = values - jnp.mean(values, axis=-1, keepdims=True)
    spread = jnp.mean(centre * centre, axis=-1, keepdims=True)
    return centre * lax.rsqrt(spread + epsilon) * gain_vec


def site_parity(patch_side):
    positions = np.arange(patch_side**4, dtype=np.int32)
    return (
        positions // patch_side**3
        + positions // patch_side**2 % patch_side
        + positions // patch_side % patch_side
        + positions % patch_side
    ) % 2


def packed_rows(p_bit):
    th, x4, y4, z4 = np.meshgrid(np.arange(2), np.arange(4), np.arange(4), np.arange(4), indexing="ij")
    t4 = 2 * th + (p_bit + x4 + y4 + z4) % 2
    return (((t4 * 4 + x4) * 4 + y4) * 4 + z4).reshape(-1)


def embed_packed(tokens, bits, w_pair, b_embed):
    both = jnp.dot(tokens, w_pair, preferred_element_type=jnp.float32)
    half = both.shape[-1] // 2
    return jnp.where(bits[..., None] > 0.5, both[..., half:], both[..., :half]) + b_embed


def shards(
    lattice_field, parity, block_list, w_embed, b_embed, gain_in, w_qkv, gain_out, w_head, b_head
):
    n_y = LY // P_SIZE
    n_z = LZ // P_SIZE
    tokens_dev = n_y * n_z
    patch_len = P_SIZE**4
    u = lattice_field
    bits = parity.reshape(n_y, n_z)

    lane = lax.broadcasted_iota(jnp.int32, u.shape, 2)
    t_pos = lax.broadcasted_iota(jnp.int32, u.shape, 0)
    x_pos = lax.broadcasted_iota(jnp.int32, u.shape, 1)
    site_bit = (t_pos + x_pos + lane // LZ + lane % LZ) % 2
    bits_lat = jnp.repeat(jnp.repeat(bits, P_SIZE, axis=0), P_SIZE, axis=1).reshape(LY * LZ)
    frozen = site_bit == bits_lat[None, None, :]
    frozen_in = jnp.where(frozen, u, 0.0).astype(jnp.bfloat16)

    packed = frozen_in[0::2] + frozen_in[1::2]
    n_off = P_SIZE * P_SIZE
    tok_ids = lax.broadcasted_iota(jnp.int32, (tokens_dev, LY * LZ), 0)
    lane_ids = lax.broadcasted_iota(jnp.int32, (tokens_dev, LY * LZ), 1)
    tok_lane = tok_ids // n_z * (P_SIZE * LZ) + tok_ids % n_z * P_SIZE
    spread_tok = (lane_ids == tok_lane).astype(jnp.bfloat16)
    packed_rows_lat = packed.reshape(2 * P_SIZE, LY * LZ)
    shifted_rows = jnp.stack(
        [
            jnp.roll(packed_rows_lat, -(k // P_SIZE * LZ + k % P_SIZE), axis=-1)
            for k in range(n_off)
        ],
        axis=1,
    ).reshape(2 * P_SIZE * n_off, LY * LZ)
    tokens = jnp.einsum(
        "fl,tl->tf", shifted_rows, spread_tok, preferred_element_type=jnp.float32
    ).astype(jnp.bfloat16)
    bits_f = bits.reshape(1, tokens_dev).astype(jnp.bfloat16)
    send = jnp.concatenate([tokens, bits_f], axis=0)
    kept, received, offsets = doubling_gather(send[None], "tm")
    slot_of = np.argsort(np.asarray(offsets)).astype(np.int32)

    w_pair = jnp.concatenate(
        [w_embed[packed_rows(0)], w_embed[packed_rows(1)]], axis=1
    )
    bits_own = bits.reshape(tokens_dev).astype(jnp.float32)
    embedded = embed_packed(tokens, bits_own, w_pair, b_embed)
    normed = layer_norm(embedded, gain_in).astype(jnp.bfloat16)

    block_rows = lax.dynamic_index_in_dim(block_list, lax.axis_index("tm"), 0, keepdims=False)
    own = lax.axis_index("tm")
    slots = jnp.asarray(slot_of)[block_rows ^ own]
    n_half = kept.shape[0]
    half_ids = jnp.arange(n_half, dtype=jnp.int32)[None, :]
    pick_kept = (slots[:, None] == half_ids).astype(jnp.bfloat16)
    pick_received = (slots[:, None] == half_ids + n_half).astype(jnp.bfloat16)
    chosen = (
        jnp.einsum("ip,pab->iab", pick_kept, kept, preferred_element_type=jnp.float32)
        + jnp.einsum("ip,pab->iab", pick_received, received, preferred_element_type=jnp.float32)
    ).astype(jnp.bfloat16)
    n_sel = chosen.shape[0]
    sel_tokens = chosen[:, :tokens_dev, :].reshape(n_sel * tokens_dev, patch_len // 2)
    sel_bits = chosen[:, tokens_dev, :].reshape(n_sel * tokens_dev).astype(jnp.float32)
    sel_embedded = embed_packed(sel_tokens, sel_bits, w_pair, b_embed)
    sel_normed = layer_norm(sel_embedded, gain_in).astype(jnp.bfloat16)
    queries = jnp.einsum(
        "tc,chd->htd", normed, w_qkv[:, :D].reshape(D, HEADS, HS),
        preferred_element_type=jnp.float32,
    ).astype(jnp.bfloat16)
    w_kv = w_qkv[:, D:].reshape(D, 2, HEADS, HS)
    kv = jnp.einsum(
        "tc,cnhd->nhtd", sel_normed, w_kv, preferred_element_type=jnp.float32
    ).astype(jnp.bfloat16)
    keys = kv[0]
    values = kv[1]

    scores = jnp.einsum(
        "hqd,hkd->hqk",
        queries,
        keys,
        preferred_element_type=jnp.float32,
    ) * HS ** (-0.5)
    row_top = jnp.max(scores, axis=-1, keepdims=True)
    exp_scores = jnp.exp(scores - row_top)
    row_total = jnp.sum(exp_scores, axis=-1)
    product = jnp.einsum(
        "hqk,hkd->qhd",
        exp_scores.astype(jnp.bfloat16),
        values,
        preferred_element_type=jnp.float32,
    )
    mixed = (product / row_total.T[:, :, None]).reshape(tokens_dev, D)
    hidden = embedded + mixed
    normed_out = layer_norm(hidden, gain_out).astype(jnp.bfloat16)
    w_rows = w_head.reshape(D, 2 * P_SIZE * P_SIZE, n_off)
    affine_rows = jnp.einsum(
        "tc,crk->krt", normed_out, w_rows, preferred_element_type=jnp.float32
    ) + b_head.reshape(2 * P_SIZE * P_SIZE, n_off).T[:, :, None]
    high = lax.reduce_precision(affine_rows, exponent_bits=8, mantissa_bits=7)
    rest = affine_rows - high
    middle = lax.reduce_precision(rest, exponent_bits=8, mantissa_bits=7)
    low = rest - middle
    pieces = jnp.concatenate([high, middle, low], axis=-1).astype(jnp.bfloat16)
    spread_three = jnp.concatenate([spread_tok, spread_tok, spread_tok], axis=0)
    affine_lanes = jnp.einsum(
        "krt,tl->krl", pieces, spread_three, preferred_element_type=jnp.float32
    )
    coupling_lat = affine_lanes[0]
    for k in range(1, n_off):
        offset = k // P_SIZE * LZ + k % P_SIZE
        coupling_lat = coupling_lat + jnp.roll(affine_lanes[k], offset, axis=-1)
    half_rows = P_SIZE * P_SIZE
    scale_lat = jnp.tanh(coupling_lat[:half_rows]).reshape(P_SIZE, P_SIZE, LY * LZ)
    shift_lat = coupling_lat[half_rows:].reshape(P_SIZE, P_SIZE, LY * LZ)
    log_det = jnp.sum(jnp.where(frozen, 0.0, scale_lat))
    new_field = jnp.where(frozen, u, u * jnp.exp(scale_lat) + shift_lat)

    ahead_time = shifted(new_field[0:1].astype(jnp.bfloat16), "tm", -1).astype(jnp.float32)
    ahead_slab = shifted(new_field[:, 0:1].astype(jnp.bfloat16), "space", -1).astype(jnp.float32)
    next_time_field = jnp.concatenate([new_field[1:], ahead_time], axis=0)
    next_slab_field = jnp.concatenate([new_field[:, 1:], ahead_slab], axis=1)
    next_y_field = jnp.roll(new_field, -LZ, axis=2)
    next_z_field = jnp.where(
        lane % LZ == LZ - 1, jnp.roll(new_field, LZ - 1, axis=2), jnp.roll(new_field, -1, axis=2)
    )
    neighbours = next_time_field + next_slab_field
    neighbours = neighbours + next_y_field
    neighbours = neighbours + next_z_field
    squared = new_field * new_field
    density = (
        -2.0 * hopping * new_field * neighbours
        + squared
        + quartic * (squared - 1.0) * (squared - 1.0)
    )
    time_link = new_field * next_time_field
    slab_link = new_field * next_slab_field
    local_log = -0.5 * jnp.sum(u * u) - log_det
    local_act = jnp.sum(density)
    members = lax.axis_size("space") * lax.axis_size("tm")
    partials = jnp.broadcast_to(jnp.stack([local_log, local_act])[None], (members, 2))
    sums = jnp.sum(lax.all_to_all(partials, ("space", "tm"), 0, 0, tiled=True), axis=0)
    sum_log, sum_act = sums[0], sums[1]
    site_count = u.size * lax.axis_size("space") * lax.axis_size("tm")
    totals = jnp.stack([sum_log / site_count - 0.5 * log_two_pi, sum_act / site_count]).astype(
        jnp.float32
    )
    return (new_field, density, time_link, slab_link, totals)


def solution(mesh):
    in_specs = (
        P("tm", "space", None),
        P("tm", "space", None),
        P(),
        P(),
        P(),
        P(),
        P(),
        P(),
        P(),
        P(),
    )
    out_specs = (
        P("tm", "space", None),
        P("tm", "space", None),
        P("tm", "space", None),
        P("tm", "space", None),
        P(),
    )
    return jax.shard_map(shards, mesh=mesh, in_specs=in_specs, out_specs=out_specs, check_vma=False)
```

```python
import math

import numpy as np
import jax
import jax.numpy as jnp
from jax import lax
from jax.sharding import PartitionSpec as P

P_SIZE = 4
D = 768
HEADS = 12
HS = 64
LY = 32
LZ = 64
BLK = 128


hopping = 0.2
quartic = 0.5
epsilon = 1e-05
log_two_pi = math.log(2.0 * math.pi)


def exchange(x, axis, bit):
    length = lax.axis_size(axis)
    return lax.ppermute(x, axis, [(i, i ^ bit) for i in range(length)])


def doubling_sum(x, axis):
    bit = 1
    while bit < lax.axis_size(axis):
        x = x + exchange(x, axis, bit)
        bit *= 2
    return x


def doubling_gather(x, axis):
    bits = []
    bit = 1
    while bit < lax.axis_size(axis):
        bits.append(bit)
        bit *= 2
    offsets = [0]
    for bit in reversed(bits[1:]):
        x = jnp.concatenate([x, exchange(x, axis, bit)], axis=0)
        offsets = offsets + [o ^ bit for o in offsets]
    received = exchange(x, axis, bits[0])
    offsets = offsets + [o ^ bits[0] for o in offsets]
    return x, received, offsets


def shifted(x, axis, by):
    length = lax.axis_size(axis)
    return lax.ppermute(x, axis, [(i, (i + by) % length) for i in range(length)])


def layer_norm(values, gain_vec):
    centre = values - jnp.mean(values, axis=-1, keepdims=True)
    spread = jnp.mean(centre * centre, axis=-1, keepdims=True)
    return centre * lax.rsqrt(spread + epsilon) * gain_vec


def site_parity(patch_side):
    positions = np.arange(patch_side**4, dtype=np.int32)
    return (
        positions // patch_side**3
        + positions // patch_side**2 % patch_side
        + positions // patch_side % patch_side
        + positions % patch_side
    ) % 2


def packed_rows(p_bit):
    th, x4, y4, z4 = np.meshgrid(np.arange(2), np.arange(4), np.arange(4), np.arange(4), indexing="ij")
    t4 = 2 * th + (p_bit + x4 + y4 + z4) % 2
    return (((t4 * 4 + x4) * 4 + y4) * 4 + z4).reshape(-1)


def embed_packed(tokens, bits, w_pair, b_embed):
    both = jnp.dot(tokens, w_pair, preferred_element_type=jnp.float32)
    half = both.shape[-1] // 2
    return jnp.where(bits[..., None] > 0.5, both[..., half:], both[..., :half]) + b_embed


def shards(
    lattice_field, parity, block_list, w_embed, b_embed, gain_in, w_qkv, gain_out, w_head, b_head
):
    n_y = LY // P_SIZE
    n_z = LZ // P_SIZE
    tokens_dev = n_y * n_z
    patch_len = P_SIZE**4
    u = lattice_field
    bits = parity.reshape(n_y, n_z)

    lane = lax.broadcasted_iota(jnp.int32, u.shape, 2)
    t_pos = lax.broadcasted_iota(jnp.int32, u.shape, 0)
    x_pos = lax.broadcasted_iota(jnp.int32, u.shape, 1)
    site_bit = (t_pos + x_pos + lane // LZ + lane % LZ) % 2
    bits_lat = jnp.repeat(jnp.repeat(bits, P_SIZE, axis=0), P_SIZE, axis=1).reshape(LY * LZ)
    frozen = site_bit == bits_lat[None, None, :]
    frozen_in = jnp.where(frozen, u, 0.0).astype(jnp.bfloat16)

    packed = frozen_in[0::2] + frozen_in[1::2]
    n_off = P_SIZE * P_SIZE
    tok_ids = lax.broadcasted_iota(jnp.int32, (tokens_dev, LY * LZ), 0)
    lane_ids = lax.broadcasted_iota(jnp.int32, (tokens_dev, LY * LZ), 1)
    tok_lane = tok_ids // n_z * (P_SIZE * LZ) + tok_ids % n_z * P_SIZE
    spread_tok = (lane_ids == tok_lane).astype(jnp.bfloat16)
    packed_rows_lat = packed.reshape(2 * P_SIZE, LY * LZ)
    shifted_rows = jnp.stack(
        [
            jnp.roll(packed_rows_lat, -(k // P_SIZE * LZ + k % P_SIZE), axis=-1)
            for k in range(n_off)
        ],
        axis=1,
    ).reshape(2 * P_SIZE * n_off, LY * LZ)
    tokens = jnp.einsum(
        "fl,tl->tf", shifted_rows, spread_tok, preferred_element_type=jnp.float32
    ).astype(jnp.bfloat16)
    bits_f = bits.reshape(1, tokens_dev).astype(jnp.bfloat16)
    send = jnp.concatenate([tokens, bits_f], axis=0)
    kept, received, offsets = doubling_gather(send[None], "tm")
    slot_of = np.argsort(np.asarray(offsets)).astype(np.int32)

    w_pair = jnp.concatenate(
        [w_embed[packed_rows(0)], w_embed[packed_rows(1)]], axis=1
    )
    bits_own = bits.reshape(tokens_dev).astype(jnp.float32)
    embedded = embed_packed(tokens, bits_own, w_pair, b_embed)
    normed = layer_norm(embedded, gain_in).astype(jnp.bfloat16)

    block_rows = lax.dynamic_index_in_dim(block_list, lax.axis_index("tm"), 0, keepdims=False)
    own = lax.axis_index("tm")
    slots = jnp.asarray(slot_of)[block_rows ^ own]
    n_half = kept.shape[0]
    half_ids = jnp.arange(n_half, dtype=jnp.int32)[None, :]
    pick_kept = (slots[:, None] == half_ids).astype(jnp.bfloat16)
    pick_received = (slots[:, None] == half_ids + n_half).astype(jnp.bfloat16)
    chosen = (
        jnp.einsum("ip,pab->iab", pick_kept, kept, preferred_element_type=jnp.float32)
        + jnp.einsum("ip,pab->iab", pick_received, received, preferred_element_type=jnp.float32)
    ).astype(jnp.bfloat16)
    n_sel = chosen.shape[0]
    sel_tokens = chosen[:, :tokens_dev, :].reshape(n_sel * tokens_dev, patch_len // 2)
    sel_bits = chosen[:, tokens_dev, :].reshape(n_sel * tokens_dev).astype(jnp.float32)
    sel_embedded = embed_packed(sel_tokens, sel_bits, w_pair, b_embed)
    sel_normed = layer_norm(sel_embedded, gain_in).astype(jnp.bfloat16)
    queries = jnp.einsum(
        "tc,chd->htd", normed, w_qkv[:, :D].reshape(D, HEADS, HS),
        preferred_element_type=jnp.float32,
    ).astype(jnp.bfloat16)
    w_kv = w_qkv[:, D:].reshape(D, 2, HEADS, HS)
    kv = jnp.einsum(
        "tc,cnhd->nhtd", sel_normed, w_kv, preferred_element_type=jnp.float32
    ).astype(jnp.bfloat16)
    keys = kv[0]
    values = kv[1]

    scores = jnp.einsum(
        "hqd,hkd->hqk",
        queries,
        keys,
        preferred_element_type=jnp.float32,
    ) * HS ** (-0.5)
    row_top = jnp.max(scores, axis=-1, keepdims=True)
    exp_scores = jnp.exp(scores - row_top)
    row_total = jnp.sum(exp_scores, axis=-1)
    product = jnp.einsum(
        "hqk,hkd->qhd",
        exp_scores.astype(jnp.bfloat16),
        values,
        preferred_element_type=jnp.float32,
    )
    mixed = (product / row_total.T[:, :, None]).reshape(tokens_dev, D)
    hidden = embedded + mixed
    normed_out = layer_norm(hidden, gain_out).astype(jnp.bfloat16)
    w_rows = w_head.reshape(D, 2 * P_SIZE * P_SIZE, n_off)
    affine_rows = jnp.dot(
        normed_out, w_head, preferred_element_type=jnp.float32
    ).reshape(tokens_dev, 2 * P_SIZE * P_SIZE, n_off).transpose(2, 1, 0) + b_head.reshape(
        2 * P_SIZE * P_SIZE, n_off
    ).T[:, :, None]
    high = lax.reduce_precision(affine_rows, exponent_bits=8, mantissa_bits=7)
    rest = affine_rows - high
    middle = lax.reduce_precision(rest, exponent_bits=8, mantissa_bits=7)
    low = rest - middle
    pieces = jnp.concatenate([high, middle, low], axis=-1).astype(jnp.bfloat16)
    spread_three = jnp.concatenate([spread_tok, spread_tok, spread_tok], axis=0)
    affine_lanes = jnp.einsum(
        "krt,tl->krl", pieces, spread_three, preferred_element_type=jnp.float32
    )
    coupling_lat = affine_lanes[0]
    for k in range(1, n_off):
        offset = k // P_SIZE * LZ + k % P_SIZE
        coupling_lat = coupling_lat + jnp.roll(affine_lanes[k], offset, axis=-1)
    half_rows = P_SIZE * P_SIZE
    scale_lat = jnp.tanh(coupling_lat[:half_rows]).reshape(P_SIZE, P_SIZE, LY * LZ)
    shift_lat = coupling_lat[half_rows:].reshape(P_SIZE, P_SIZE, LY * LZ)
    log_det = jnp.sum(jnp.where(frozen, 0.0, scale_lat))
    new_field = jnp.where(frozen, u, u * jnp.exp(scale_lat) + shift_lat)

    ahead_time = shifted(new_field[0:1].astype(jnp.bfloat16), "tm", -1).astype(jnp.float32)
    ahead_slab = shifted(new_field[:, 0:1].astype(jnp.bfloat16), "space", -1).astype(jnp.float32)
    next_time_field = jnp.concatenate([new_field[1:], ahead_time], axis=0)
    next_slab_field = jnp.concatenate([new_field[:, 1:], ahead_slab], axis=1)
    next_y_field = jnp.roll(new_field, -LZ, axis=2)
    next_z_field = jnp.where(
        lane % LZ == LZ - 1, jnp.roll(new_field, LZ - 1, axis=2), jnp.roll(new_field, -1, axis=2)
    )
    neighbours = next_time_field + next_slab_field
    neighbours = neighbours + next_y_field
    neighbours = neighbours + next_z_field
    squared = new_field * new_field
    density = (
        -2.0 * hopping * new_field * neighbours
        + squared
        + quartic * (squared - 1.0) * (squared - 1.0)
    )
    time_link = new_field * next_time_field
    slab_link = new_field * next_slab_field
    local_log = -0.5 * jnp.sum(u * u) - log_det
    local_act = jnp.sum(density)
    members = lax.axis_size("space") * lax.axis_size("tm")
    partials = jnp.broadcast_to(jnp.stack([local_log, local_act])[None], (members, 2))
    sums = jnp.sum(lax.all_to_all(partials, ("space", "tm"), 0, 0, tiled=True), axis=0)
    sum_log, sum_act = sums[0], sums[1]
    site_count = u.size * lax.axis_size("space") * lax.axis_size("tm")
    totals = jnp.stack([sum_log / site_count - 0.5 * log_two_pi, sum_act / site_count]).astype(
        jnp.float32
    )
    return (new_field, density, time_link, slab_link, totals)


def solution(mesh):
    in_specs = (
        P("tm", "space", None),
        P("tm", "space", None),
        P(),
        P(),
        P(),
        P(),
        P(),
        P(),
        P(),
        P(),
    )
    out_specs = (
        P("tm", "space", None),
        P("tm", "space", None),
        P("tm", "space", None),
        P("tm", "space", None),
        P(),
    )
    return jax.shard_map(shards, mesh=mesh, in_specs=in_specs, out_specs=out_specs, check_vma=False)
```
